256 devices in a mesh: ctx: 32 (over y, z_hi, x), uly: 8 (over z_lo, core).
Axes of the slice: x: 4, y: 4, z: 8 (z_hi: 2, z_lo: 4; z = z_hi * 4 + z_lo), core: 2. Of those that a mesh axis runs over, the one named last changes fastest.
Arguments:
- queries: bfloat16 [32768, 4096], P(('ctx', 'uly')), may hold values from -5 to 5
- keys: bfloat16 [32768, 1024], P(('ctx', 'uly')), may hold values from -5 to 5
- values: bfloat16 [32768, 1024], P(('ctx', 'uly')), may hold values from -6 to 6
- output_gradient: bfloat16 [32768, 4096], P(('ctx', 'uly')), may hold values from -6 to 6
- doc_lengths: int32 [32], replicated, may hold values from 1 to 3072, 32768 in all
Outputs:
- grad_queries: bfloat16 [32768, 4096], P(('ctx', 'uly'))
- keys_gradient: bfloat16 [32768, 1024], P(('ctx', 'uly'))
- values_gradient: bfloat16 [32768, 1024], P(('ctx', 'uly'))
The draws below stay inside these ranges and needn't reach their ends.
Inputs may be any that keep to these rules, and one draw needn't show every extreme that they name: `doc_lengths`: whole documents that fill the sequence; the longest is exactly 3072 tokens.
All inputs are finite; a program needn't handle non-finite values.
Results may differ from the reference program's by a relative error of at most 0.017.
Values may be sent and summed in bfloat16 or wider, within the bound.
No kernel may reach another device: no remote copies, remote signals or barrier semaphores. Data moves between devices by JAX's collectives and lax.ppermute only.
A program may use at most 64 MiB of HBM per device.

```python
import math
import jax
import jax.numpy as jnp
import numpy as np
from jax import lax

QUERY_HEADS = 32
KEY_VALUE_HEADS = 8
HEAD_SIZE = 128
NDOCS = 32
SHARD = 1024
PACKED_TOKENS = 32768
MOST = 3072


def draw_queries(key, part):
    normal_samples = jax.random.normal(jax.random.fold_in(key, 2), (PACKED_TOKENS, QUERY_HEADS * HEAD_SIZE), jnp.float32)
    return jnp.clip(normal_samples, -5.0, 5.0).astype(jnp.bfloat16)


def draw_keys(key, part):
    normal_samples = jax.random.normal(jax.random.fold_in(key, 4), (PACKED_TOKENS, KEY_VALUE_HEADS * HEAD_SIZE), jnp.float32)
    return jnp.clip(normal_samples, -5.0, 5.0).astype(jnp.bfloat16)


def steps_of(rng, extent, cuts, low, largest):
    def one(axis_at, shards_of):
        heights = jax.random.uniform(jax.random.fold_in(jax.random.fold_in(rng, 6), axis_at), (shards_of,), jnp.float32, low / len(cuts), largest / len(cuts))
        return jnp.repeat(jnp.exp(heights), extent[axis_at] // shards_of).reshape((-1,) + (1,) * (len(extent) - axis_at - 1))

    gain = one(*cuts[0])
    for cut in cuts[1:]:
        gain = gain * one(*cut)
    return gain


def length_profile(amount, total, reach, skew):
    weights = [(1 << 20) // math.isqrt(grade ** skew) + 1 for grade in range(2, amount + 1)]
    surplus, counts = total - reach - (amount - 1), [1] * (amount - 1)
    while surplus > 0:
        movable = [i for i in range(amount - 1) if counts[i] < reach]
        whole, remaining = sum([weights[i] for i in movable]), surplus
        for i in movable:
            addition = min(reach - counts[i], max(1, remaining * weights[i] // whole), surplus)
            counts[i] = counts[i] + addition
            surplus = surplus - addition
    return np.array([reach] + counts)


def ragged_sizes(own_key, number_of, total, most, slope):
    if number_of == 2:
        one = jax.random.randint(own_key, (), max(1, total - most), min(most, total - 1) + 1)
        return jnp.stack([one, total - one])
    sizes = jnp.asarray(length_profile(number_of, total, most, slope), jnp.int32)
    twos = (number_of - 1) // 2
    giver, receiver = sizes[1:1 + 2 * twos:2], sizes[2:2 + 2 * twos:2]
    slack = jnp.minimum(giver - 1, most - receiver)
    passed = jax.random.randint(jax.random.fold_in(own_key, 1), (twos,), 0, 1 << 20) % (slack + 1)
    sizes = sizes.at[1:1 + 2 * twos:2].set(giver - passed).at[2:2 + 2 * twos:2].set(receiver + passed)
    return sizes[jax.random.permutation(jax.random.fold_in(own_key, 2), number_of)]


def bell_draw(stream_key, shape, scale, reach, cuts=(), kind=jnp.bfloat16):
    gain = steps_of(stream_key, shape, cuts, -0.22, 0.18) if cuts else 1.0
    result = jax.random.normal(stream_key, shape, jnp.float32) * scale * gain
    return jnp.minimum(jnp.maximum(result, -reach), reach).astype(kind)


def setup_inputs(seed: int = 0) -> dict:
    splits = jax.random.split(jax.random.key(seed), 6)
    queries = draw_queries(jax.random.fold_in(splits[5], 71), 0)
    keys = draw_keys(jax.random.fold_in(splits[5], 71), 0)
    values = bell_draw(splits[2], (PACKED_TOKENS, KEY_VALUE_HEADS * HEAD_SIZE), 1.0, 6.0, ((0, 256),))
    output_gradient = bell_draw(splits[3], (PACKED_TOKENS, QUERY_HEADS * HEAD_SIZE), 1.0, 6.0, ((0, 256),))
    doc_lengths = ragged_sizes(splits[4], NDOCS, PACKED_TOKENS, MOST, 1).astype(jnp.int32)
    return dict(queries=queries, keys=keys, values=values, output_gradient=output_gradient, doc_lengths=doc_lengths)


NEG = -1e+30

def reference(queries, keys, values, output_gradient, doc_lengths):
    group_members = QUERY_HEADS // KEY_VALUE_HEADS
    softmax_scale = 1.0 / math.sqrt(HEAD_SIZE)
    block = math.gcd(SHARD, 256)
    width = MOST + block
    ends = jnp.cumsum(doc_lengths).astype(jnp.int32)
    query_four = queries.astype(jnp.float32).reshape(PACKED_TOKENS, KEY_VALUE_HEADS, group_members, HEAD_SIZE)
    gradient_four = output_gradient.astype(jnp.float32).reshape(PACKED_TOKENS, KEY_VALUE_HEADS, group_members, HEAD_SIZE)
    key_three = keys.astype(jnp.float32).reshape(PACKED_TOKENS, KEY_VALUE_HEADS, HEAD_SIZE)
    value_three = values.astype(jnp.float32).reshape(PACKED_TOKENS, KEY_VALUE_HEADS, HEAD_SIZE)

    def one_block(carry, index):
        key_gradient, value_gradient = carry
        q_first = (index * block).astype(jnp.int32)
        w_first = jnp.maximum(q_first - MOST, 0).astype(jnp.int32)
        q_tile = lax.dynamic_slice_in_dim(query_four, q_first, block, 0)
        g_tile = lax.dynamic_slice_in_dim(gradient_four, q_first, block, 0)
        k_tile = lax.dynamic_slice_in_dim(key_three, w_first, width, 0)
        v_tile = lax.dynamic_slice_in_dim(value_three, w_first, width, 0)
        q_pos = q_first + jnp.arange(block, dtype=jnp.int32)
        k_pos = w_first + jnp.arange(width, dtype=jnp.int32)
        q_start = lax.optimization_barrier(jnp.sum(jnp.where(ends[None, :] <= q_pos[:, None], doc_lengths[None, :], 0), axis=1)).astype(jnp.int32)
        mask = (k_pos[None, :] <= q_pos[:, None]) & (k_pos[None, :] >= q_start[:, None])
        raw = jnp.einsum('qhgd,khd->hgqk', q_tile, k_tile) * softmax_scale
        scores = jnp.where(mask[None, None], raw, NEG)
        high = lax.optimization_barrier(jnp.max(scores, axis=3))
        shifted = jnp.where(mask[None, None], jnp.exp(scores - high[..., None]), 0.0)
        total = lax.optimization_barrier(jnp.sum(shifted, axis=3))
        lse = high + jnp.log(total)
        weights = lax.optimization_barrier(shifted.astype(jnp.bfloat16)).astype(jnp.float32)
        attn = jnp.einsum('hgqk,khd->qhgd', weights, v_tile) / jnp.transpose(total, (2, 0, 1))[..., None]
        attn_b = lax.optimization_barrier(attn.astype(jnp.bfloat16)).astype(jnp.float32)
        probs = jnp.where(mask[None, None], jnp.exp(scores - lse[..., None]), 0.0)
        probs_b = lax.optimization_barrier(probs.astype(jnp.bfloat16)).astype(jnp.float32)
        delta = jnp.transpose(lax.optimization_barrier(jnp.sum(g_tile * attn_b, axis=3)), (1, 2, 0))
        dprobs = jnp.einsum('qhgd,khd->hgqk', g_tile, v_tile)
        dscores = lax.optimization_barrier((probs * (dprobs - delta[..., None])).astype(jnp.bfloat16)).astype(jnp.float32)
        grad_q = (softmax_scale * jnp.einsum('hgqk,khd->qhgd', dscores, k_tile)).astype(jnp.bfloat16).reshape(block, QUERY_HEADS * HEAD_SIZE)
        part_k = jnp.einsum('hgqk,qhgd->khd', dscores, q_tile)
        part_v = jnp.einsum('hgqk,qhgd->khd', probs_b, g_tile)
        key_gradient = lax.dynamic_update_slice_in_dim(key_gradient, lax.dynamic_slice_in_dim(key_gradient, w_first, width, 0) + part_k, w_first, 0)
        value_gradient = lax.dynamic_update_slice_in_dim(value_gradient, lax.dynamic_slice_in_dim(value_gradient, w_first, width, 0) + part_v, w_first, 0)
        return ((key_gradient, value_gradient), grad_q)
    zero_filled = jnp.zeros((PACKED_TOKENS, KEY_VALUE_HEADS, HEAD_SIZE), jnp.float32)
    (key_gradient, value_gradient), blocks = lax.scan(one_block, (zero_filled, zero_filled), jnp.arange(PACKED_TOKENS // block, dtype=jnp.int32))
    grad_queries = blocks.reshape(PACKED_TOKENS, QUERY_HEADS * HEAD_SIZE)
    keys_gradient = (softmax_scale * key_gradient).astype(jnp.bfloat16).reshape(PACKED_TOKENS, KEY_VALUE_HEADS * HEAD_SIZE)
    values_gradient = value_gradient.astype(jnp.bfloat16).reshape(PACKED_TOKENS, KEY_VALUE_HEADS * HEAD_SIZE)
    return (grad_queries, keys_gradient, values_gradient)
```

```python
import functools
import math

import jax
import jax.numpy as jnp
from jax import lax
from jax.experimental import pallas as pl
from jax.experimental.pallas import tpu as pltpu
from jax.sharding import PartitionSpec as P

HEAD_SIZE = 128
REACH = 3
Q_BLOCK = 256
K_BLOCK = 512

NEG = -1e30


def from_behind(shard, axis, by):
    length = lax.axis_size(axis)
    pairs = [(i, i + by) for i in range(length) if 0 <= i + by < length]
    return lax.ppermute(shard, axis, pairs)


def attention_kernel(
    meta_ref, q_ref, do_ref, k_ref, v_ref, qs_ref,
    dq_ref, dk_ref, dv_ref,
    m_s, l_s, acc_s, lse_s, delta_s, dq_s,
    *, groups, q_blocks, scale,
):
    T, TK, D = Q_BLOCK, K_BLOCK, HEAD_SIZE
    dk_ref[...] = jnp.zeros_like(dk_ref)
    dv_ref[...] = jnp.zeros_like(dv_ref)
    q_base = meta_ref[0]
    k_base = meta_ref[1]

    def tile_mask(q0, kb):
        q_pos = q_base + q0 + lax.broadcasted_iota(jnp.int32, (T, TK), 0)
        k_pos = k_base + kb * TK + lax.broadcasted_iota(jnp.int32, (T, TK), 1)
        start = qs_ref[pl.ds(q0, T), :]
        return (k_pos <= q_pos) & (k_pos >= start)

    def q_block(qb, carry):
        q0 = pl.multiple_of(qb * T, T)
        lo = meta_ref[2 + 2 * qb]
        hi = meta_ref[3 + 2 * qb]
        m_s[...] = jnp.full_like(m_s, NEG)
        l_s[...] = jnp.zeros_like(l_s)
        acc_s[...] = jnp.zeros_like(acc_s)

        def fwd(kb, c):
            k0 = pl.multiple_of(kb * TK, TK)
            k = k_ref[pl.ds(k0, TK), :]
            v = v_ref[pl.ds(k0, TK), :]
            mask = tile_mask(q0, kb)
            for h in range(groups):
                qh = q_ref[pl.ds(q0, T), pl.ds(h * D, D)]
                raw = lax.dot_general(
                    qh, k, (((1,), (1,)), ((), ())), preferred_element_type=jnp.float32
                ) * scale
                s = jnp.where(mask, raw, NEG)
                old_high = m_s[h]
                new_high = jnp.maximum(old_high, jnp.max(s, axis=1, keepdims=True))
                factor = jnp.exp(old_high - new_high)
                terms = jnp.where(mask, jnp.exp(s - new_high), 0.0)
                l_s[h] = l_s[h] * factor + jnp.sum(terms, axis=1, keepdims=True)
                acc_s[h] = acc_s[h] * factor + jnp.dot(
                    terms.astype(jnp.bfloat16), v, preferred_element_type=jnp.float32
                )
                m_s[h] = new_high
            return c

        lax.fori_loop(lo, hi, fwd, 0)
        for h in range(groups):
            total = l_s[h]
            lse_s[h] = m_s[h] + jnp.log(total)
            out = (acc_s[h] / total).astype(jnp.bfloat16).astype(jnp.float32)
            g = do_ref[pl.ds(q0, T), pl.ds(h * D, D)].astype(jnp.float32)
            delta_s[h] = jnp.sum(g * out, axis=1, keepdims=True)
        dq_s[...] = jnp.zeros_like(dq_s)

        def bwd(kb, c):
            k0 = pl.multiple_of(kb * TK, TK)
            k = k_ref[pl.ds(k0, TK), :]
            v = v_ref[pl.ds(k0, TK), :]
            mask = tile_mask(q0, kb)
            add_k = jnp.zeros((TK, D), jnp.float32)
            add_v = jnp.zeros((TK, D), jnp.float32)
            for h in range(groups):
                qh = q_ref[pl.ds(q0, T), pl.ds(h * D, D)]
                gh = do_ref[pl.ds(q0, T), pl.ds(h * D, D)]
                raw = lax.dot_general(
                    qh, k, (((1,), (1,)), ((), ())), preferred_element_type=jnp.float32
                ) * scale
                s = jnp.where(mask, raw, NEG)
                probs = jnp.where(mask, jnp.exp(s - lse_s[h]), 0.0)
                dprobs = lax.dot_general(
                    gh, v, (((1,), (1,)), ((), ())), preferred_element_type=jnp.float32
                )
                dscores = probs * (dprobs - delta_s[h])
                dq_s[h] = dq_s[h] + jnp.dot(
                    dscores.astype(jnp.bfloat16), k, preferred_element_type=jnp.float32
                )
                add_k = add_k + jnp.dot(
                    dscores.T.astype(jnp.bfloat16), qh, preferred_element_type=jnp.float32
                )
                add_v = add_v + jnp.dot(
                    probs.T.astype(jnp.bfloat16), gh, preferred_element_type=jnp.float32
                )
            dk_ref[pl.ds(k0, TK), :] = dk_ref[pl.ds(k0, TK), :] + add_k
            dv_ref[pl.ds(k0, TK), :] = dv_ref[pl.ds(k0, TK), :] + add_v
            return c

        lax.fori_loop(lo, hi, bwd, 0)
        for h in range(groups):
            dq_ref[pl.ds(q0, T), pl.ds(h * D, D)] = (scale * dq_s[h]).astype(dq_ref.dtype)
        return carry

    lax.fori_loop(0, q_blocks, q_block, 0)


def attend(meta, queries, gradient, key_window, value_window, q_start, groups, scale):
    rows = queries.shape[0]
    width = key_window.shape[0]
    q_blocks = rows // Q_BLOCK
    vmem = pltpu.MemorySpace.VMEM
    kernel = functools.partial(
        attention_kernel, groups=groups, q_blocks=q_blocks, scale=scale
    )
    return pl.pallas_call(
        kernel,
        out_shape=(
            jax.ShapeDtypeStruct(queries.shape, jnp.bfloat16),
            jax.ShapeDtypeStruct((width, HEAD_SIZE), jnp.float32),
            jax.ShapeDtypeStruct((width, HEAD_SIZE), jnp.float32),
        ),
        in_specs=[pl.BlockSpec(memory_space=pltpu.MemorySpace.SMEM)]
        + [pl.BlockSpec(memory_space=vmem)] * 5,
        out_specs=[pl.BlockSpec(memory_space=vmem)] * 3,
        scratch_shapes=[
            pltpu.VMEM((groups, Q_BLOCK, 1), jnp.float32),
            pltpu.VMEM((groups, Q_BLOCK, 1), jnp.float32),
            pltpu.VMEM((groups, Q_BLOCK, HEAD_SIZE), jnp.float32),
            pltpu.VMEM((groups, Q_BLOCK, 1), jnp.float32),
            pltpu.VMEM((groups, Q_BLOCK, 1), jnp.float32),
            pltpu.VMEM((groups, Q_BLOCK, HEAD_SIZE), jnp.float32),
        ],
        compiler_params=pltpu.CompilerParams(vmem_limit_bytes=48 * 1024 * 1024),
    )(meta, queries, gradient, key_window, value_window, q_start)


def on_device(queries, keys, values, output_gradient, doc_lengths):
    uly = lax.axis_size("uly")
    tokens = queries.shape[0]
    q_cols = queries.shape[1] // uly
    kv_cols = keys.shape[1] // uly
    packed = jnp.concatenate(
        [
            queries.reshape(tokens, uly, q_cols),
            output_gradient.reshape(tokens, uly, q_cols),
            keys.reshape(tokens, uly, kv_cols),
            values.reshape(tokens, uly, kv_cols),
        ],
        axis=2,
    )
    packed = lax.all_to_all(packed, "uly", split_axis=1, concat_axis=0, tiled=True)
    rows = packed.shape[0]
    packed = packed.reshape(rows, 2 * q_cols + 2 * kv_cols)
    queries = packed[:, :q_cols]
    gradient = packed[:, q_cols : 2 * q_cols]
    kv = packed[:, 2 * q_cols :]
    groups = q_cols // HEAD_SIZE
    softmax_scale = 1.0 / math.sqrt(HEAD_SIZE)

    window = [kv]
    for step in range(1, REACH + 1):
        window.append(from_behind(kv, "ctx", step))
    window = jnp.concatenate(window[::-1], axis=0)
    key_window = window[:, :HEAD_SIZE]
    value_window = window[:, HEAD_SIZE:]

    ctx_index = lax.axis_index("ctx")
    q_base = ctx_index * rows
    k_base = (ctx_index - REACH) * rows
    q_pos = q_base + jnp.arange(rows, dtype=jnp.int32)
    ends = jnp.cumsum(doc_lengths)
    q_start = jnp.sum(
        jnp.where(ends[None, :] <= q_pos[:, None], doc_lengths[None, :], 0), axis=1
    ).astype(jnp.int32)
    first_rows = jnp.arange(0, rows, Q_BLOCK, dtype=jnp.int32)
    lo = jnp.maximum((q_start[first_rows] - k_base) // K_BLOCK, 0)
    hi = (q_base + first_rows + Q_BLOCK - 1 - k_base) // K_BLOCK + 1
    meta = jnp.concatenate(
        [jnp.stack([q_base, k_base]).astype(jnp.int32), jnp.stack([lo, hi], axis=1).reshape(-1)]
    ).astype(jnp.int32)

    dq, dk_window, dv_window = attend(
        meta, queries, gradient, key_window, value_window, q_start[:, None], groups, softmax_scale
    )
    partials = jnp.concatenate([dk_window, dv_window], axis=1)
    total = partials[REACH * rows :]
    for step in range(1, REACH + 1):
        piece = partials[(REACH - step) * rows : (REACH - step + 1) * rows]
        total = total + from_behind(piece.astype(jnp.bfloat16), "ctx", -step).astype(jnp.float32)
    out_k = (softmax_scale * total[:, :HEAD_SIZE]).astype(jnp.bfloat16)
    out_v = total[:, HEAD_SIZE:].astype(jnp.bfloat16)
    result = jnp.concatenate([dq, out_k, out_v], axis=1)
    result = lax.all_to_all(result, "uly", split_axis=0, concat_axis=1, tiled=True)
    piece_cols = q_cols + 2 * kv_cols
    result = result.reshape(result.shape[0], uly, piece_cols)
    return (
        result[:, :, :q_cols].reshape(result.shape[0], uly * q_cols),
        result[:, :, q_cols : q_cols + kv_cols].reshape(result.shape[0], uly * kv_cols),
        result[:, :, q_cols + kv_cols :].reshape(result.shape[0], uly * kv_cols),
    )


def solution(mesh):
    return jax.shard_map(
        on_device,
        mesh=mesh,
        in_specs=(
            P(("ctx", "uly"), None),
            P(("ctx", "uly"), None),
            P(("ctx", "uly"), None),
            P(("ctx", "uly"), None),
            P(),
        ),
        out_specs=(P(("ctx", "uly"), None), P(("ctx", "uly"), None), P(("ctx", "uly"), None)),
        check_vma=False,
    )
```

```python
import functools
import math

import jax
import jax.numpy as jnp
from jax import lax
from jax.experimental import pallas as pl
from jax.experimental.pallas import tpu as pltpu
from jax.sharding import PartitionSpec as P

HEAD_SIZE = 128
REACH = 3
Q_BLOCK = 256
K_BLOCK = 512

NEG = -1e30


def mirror_of(uly, cores):
    run = uly // cores
    return [(run - 1 - u // cores) * cores + u % cores for u in range(uly)]


def from_behind(shard, by, flips, cores):
    ctx = lax.axis_size("ctx")
    uly = lax.axis_size("uly")
    mirror = mirror_of(uly, cores)
    pairs = []
    for c in range(ctx):
        d = c + by
        if not 0 <= d < ctx:
            continue
        for u in range(uly):
            group = mirror[u] if flips[c] else u
            pairs.append((c * uly + u, d * uly + (mirror[group] if flips[d] else group)))
    return lax.ppermute(shard, ("ctx", "uly"), pairs)


def mirrored(x, flip, cores):
    rows, uly = x.shape[0], x.shape[1]
    split = x.reshape(rows, uly // cores, cores, x.shape[2])
    return jnp.where(flip, split[:, ::-1], split).reshape(x.shape)


def attention_kernel(
    meta_ref, q_ref, do_ref, k_ref, v_ref, qs_ref,
    dq_ref, dk_ref, dv_ref,
    m_s, l_s, acc_s, lse_s, delta_s, dq_s,
    *, groups, q_blocks, scale,
):
    T, TK, D = Q_BLOCK, K_BLOCK, HEAD_SIZE
    dk_ref[...] = jnp.zeros_like(dk_ref)
    dv_ref[...] = jnp.zeros_like(dv_ref)
    q_base = meta_ref[0]
    k_base = meta_ref[1]

    def tile_mask(q0, kb):
        q_pos = q_base + q0 + lax.broadcasted_iota(jnp.int32, (T, TK), 0)
        k_pos = k_base + kb * TK + lax.broadcasted_iota(jnp.int32, (T, TK), 1)
        start = qs_ref[pl.ds(q0, T), :]
        return (k_pos <= q_pos) & (k_pos >= start)

    def q_block(qb, carry):
        q0 = pl.multiple_of(qb * T, T)
        lo = meta_ref[2 + 2 * qb]
        hi = meta_ref[3 + 2 * qb]
        m_s[...] = jnp.full_like(m_s, NEG)
        l_s[...] = jnp.zeros_like(l_s)
        acc_s[...] = jnp.zeros_like(acc_s)

        def fwd(kb, c):
            k0 = pl.multiple_of(kb * TK, TK)
            k = k_ref[pl.ds(k0, TK), :]
            v = v_ref[pl.ds(k0, TK), :]
            mask = tile_mask(q0, kb)
            for h in range(groups):
                qh = q_ref[pl.ds(q0, T), pl.ds(h * D, D)]
                raw = lax.dot_general(
                    qh, k, (((1,), (1,)), ((), ())), preferred_element_type=jnp.float32
                ) * scale
                s = jnp.where(mask, raw, NEG)
                old_high = m_s[h]
                new_high = jnp.maximum(old_high, jnp.max(s, axis=1, keepdims=True))
                factor = jnp.exp(old_high - new_high)
                terms = jnp.where(mask, jnp.exp(s - new_high), 0.0)
                l_s[h] = l_s[h] * factor + jnp.sum(terms, axis=1, keepdims=True)
                acc_s[h] = acc_s[h] * factor + jnp.dot(
                    terms.astype(jnp.bfloat16), v, preferred_element_type=jnp.float32
                )
                m_s[h] = new_high
            return c

        lax.fori_loop(lo, hi, fwd, 0)
        for h in range(groups):
            total = l_s[h]
            lse_s[h] = m_s[h] + jnp.log(total)
            out = (acc_s[h] / total).astype(jnp.bfloat16).astype(jnp.float32)
            g = do_ref[pl.ds(q0, T), pl.ds(h * D, D)].astype(jnp.float32)
            delta_s[h] = jnp.sum(g * out, axis=1, keepdims=True)
        dq_s[...] = jnp.zeros_like(dq_s)

        def bwd(kb, c):
            k0 = pl.multiple_of(kb * TK, TK)
            k = k_ref[pl.ds(k0, TK), :]
            v = v_ref[pl.ds(k0, TK), :]
            mask = tile_mask(q0, kb)
            add_k = jnp.zeros((TK, D), jnp.float32)
            add_v = jnp.zeros((TK, D), jnp.float32)
            for h in range(groups):
                qh = q_ref[pl.ds(q0, T), pl.ds(h * D, D)]
                gh = do_ref[pl.ds(q0, T), pl.ds(h * D, D)]
                raw = lax.dot_general(
                    qh, k, (((1,), (1,)), ((), ())), preferred_element_type=jnp.float32
                ) * scale
                s = jnp.where(mask, raw, NEG)
                probs = jnp.where(mask, jnp.exp(s - lse_s[h]), 0.0)
                dprobs = lax.dot_general(
                    gh, v, (((1,), (1,)), ((), ())), preferred_element_type=jnp.float32
                )
                dscores = probs * (dprobs - delta_s[h])
                dq_s[h] = dq_s[h] + jnp.dot(
                    dscores.astype(jnp.bfloat16), k, preferred_element_type=jnp.float32
                )
                add_k = add_k + jnp.dot(
                    dscores.T.astype(jnp.bfloat16), qh, preferred_element_type=jnp.float32
                )
                add_v = add_v + jnp.dot(
                    probs.T.astype(jnp.bfloat16), gh, preferred_element_type=jnp.float32
                )
            dk_ref[pl.ds(k0, TK), :] = dk_ref[pl.ds(k0, TK), :] + add_k
            dv_ref[pl.ds(k0, TK), :] = dv_ref[pl.ds(k0, TK), :] + add_v
            return c

        lax.fori_loop(lo, hi, bwd, 0)
        for h in range(groups):
            dq_ref[pl.ds(q0, T), pl.ds(h * D, D)] = (scale * dq_s[h]).astype(dq_ref.dtype)
        return carry

    lax.fori_loop(0, q_blocks, q_block, 0)


def attend(meta, queries, gradient, key_window, value_window, q_start, groups, scale):
    rows = queries.shape[0]
    width = key_window.shape[0]
    q_blocks = rows // Q_BLOCK
    vmem = pltpu.MemorySpace.VMEM
    kernel = functools.partial(
        attention_kernel, groups=groups, q_blocks=q_blocks, scale=scale
    )
    return pl.pallas_call(
        kernel,
        out_shape=(
            jax.ShapeDtypeStruct(queries.shape, jnp.bfloat16),
            jax.ShapeDtypeStruct((width, HEAD_SIZE), jnp.float32),
            jax.ShapeDtypeStruct((width, HEAD_SIZE), jnp.float32),
        ),
        in_specs=[pl.BlockSpec(memory_space=pltpu.MemorySpace.SMEM)]
        + [pl.BlockSpec(memory_space=vmem)] * 5,
        out_specs=[pl.BlockSpec(memory_space=vmem)] * 3,
        scratch_shapes=[
            pltpu.VMEM((groups, Q_BLOCK, 1), jnp.float32),
            pltpu.VMEM((groups, Q_BLOCK, 1), jnp.float32),
            pltpu.VMEM((groups, Q_BLOCK, HEAD_SIZE), jnp.float32),
            pltpu.VMEM((groups, Q_BLOCK, 1), jnp.float32),
            pltpu.VMEM((groups, Q_BLOCK, 1), jnp.float32),
            pltpu.VMEM((groups, Q_BLOCK, HEAD_SIZE), jnp.float32),
        ],
        compiler_params=pltpu.CompilerParams(vmem_limit_bytes=48 * 1024 * 1024),
    )(meta, queries, gradient, key_window, value_window, q_start)


def on_device(queries, keys, values, output_gradient, doc_lengths, flips, cores):
    uly = lax.axis_size("uly")
    ctx_index = lax.axis_index("ctx")
    flip = jnp.asarray(flips)[ctx_index]
    tokens = queries.shape[0]
    q_cols = queries.shape[1] // uly
    kv_cols = keys.shape[1] // uly
    packed = jnp.concatenate(
        [
            queries.reshape(tokens, uly, q_cols),
            output_gradient.reshape(tokens, uly, q_cols),
            keys.reshape(tokens, uly, kv_cols),
            values.reshape(tokens, uly, kv_cols),
        ],
        axis=2,
    )
    packed = mirrored(packed, flip, cores)
    packed = lax.all_to_all(packed, "uly", split_axis=1, concat_axis=0, tiled=True)
    rows = packed.shape[0]
    packed = packed.reshape(rows, 2 * q_cols + 2 * kv_cols)
    queries = packed[:, :q_cols]
    gradient = packed[:, q_cols : 2 * q_cols]
    kv = packed[:, 2 * q_cols :]
    groups = q_cols // HEAD_SIZE
    softmax_scale = 1.0 / math.sqrt(HEAD_SIZE)

    window = [kv]
    for step in range(1, REACH + 1):
        window.append(from_behind(kv, step, flips, cores))
    window = jnp.concatenate(window[::-1], axis=0)
    key_window = window[:, :HEAD_SIZE]
    value_window = window[:, HEAD_SIZE:]

    q_base = ctx_index * rows
    k_base = (ctx_index - REACH) * rows
    q_pos = q_base + jnp.arange(rows, dtype=jnp.int32)
    ends = jnp.cumsum(doc_lengths)
    q_start = jnp.sum(
        jnp.where(ends[None, :] <= q_pos[:, None], doc_lengths[None, :], 0), axis=1
    ).astype(jnp.int32)
    first_rows = jnp.arange(0, rows, Q_BLOCK, dtype=jnp.int32)
    lo = jnp.maximum((q_start[first_rows] - k_base) // K_BLOCK, 0)
    hi = (q_base + first_rows + Q_BLOCK - 1 - k_base) // K_BLOCK + 1
    meta = jnp.concatenate(
        [jnp.stack([q_base, k_base]).astype(jnp.int32), jnp.stack([lo, hi], axis=1).reshape(-1)]
    ).astype(jnp.int32)

    dq, dk_window, dv_window = attend(
        meta, queries, gradient, key_window, value_window, q_start[:, None], groups, softmax_scale
    )
    partials = jnp.concatenate([dk_window, dv_window], axis=1)
    total = partials[REACH * rows :]
    for step in range(1, REACH + 1):
        piece = partials[(REACH - step) * rows : (REACH - step + 1) * rows]
        total = total + from_behind(piece.astype(jnp.bfloat16), -step, flips, cores).astype(jnp.float32)
    out_k = (softmax_scale * total[:, :HEAD_SIZE]).astype(jnp.bfloat16)
    out_v = total[:, HEAD_SIZE:].astype(jnp.bfloat16)
    result = jnp.concatenate([dq, out_k, out_v], axis=1)
    result = lax.all_to_all(result, "uly", split_axis=0, concat_axis=1, tiled=True)
    piece_cols = q_cols + 2 * kv_cols
    result = mirrored(result.reshape(result.shape[0], uly, piece_cols), flip, cores)
    return (
        result[:, :, :q_cols].reshape(result.shape[0], uly * q_cols),
        result[:, :, q_cols : q_cols + kv_cols].reshape(result.shape[0], uly * kv_cols),
        result[:, :, q_cols + kv_cols :].reshape(result.shape[0], uly * kv_cols),
    )


def layout_of(mesh):
    devices = mesh.devices
    cores = len({getattr(d, "core_on_chip", 0) for d in devices.flat})
    run = devices.shape[1] // cores
    coords = [getattr(devices[c, 0], "coords", None) for c in range(devices.shape[0])]
    if any(xyz is None for xyz in coords):
        return (False,) * devices.shape[0], cores
    return tuple(bool((xyz[2] // run) % 2) for xyz in coords), cores


def solution(mesh):
    flips, cores = layout_of(mesh)
    return jax.shard_map(
        functools.partial(on_device, flips=flips, cores=cores),
        mesh=mesh,
        in_specs=(
            P(("ctx", "uly"), None),
            P(("ctx", "uly"), None),
            P(("ctx", "uly"), None),
            P(("ctx", "uly"), None),
            P(),
        ),
        out_specs=(P(("ctx", "uly"), None), P(("ctx", "uly"), None), P(("ctx", "uly"), None)),
        check_vma=False,
    )
```

```python
import functools
import math

import jax
import jax.numpy as jnp
from jax import lax
from jax.experimental import pallas as pl
from jax.experimental.pallas import tpu as pltpu
from jax.sharding import PartitionSpec as P

HEAD_SIZE = 128
REACH = 3
Q_BLOCK = 256
K_BLOCK = 512

NEG = -1e30


def mirror_of(uly, cores):
    run = uly // cores
    return [(run - 1 - u // cores) * cores + u % cores for u in range(uly)]


def from_behind(shard, by, flips, cores):
    ctx = lax.axis_size("ctx")
    uly = lax.axis_size("uly")
    mirror = mirror_of(uly, cores)
    pairs = []
    for c in range(ctx):
        d = c + by
        if not 0 <= d < ctx:
            continue
        for u in range(uly):
            group = mirror[u] if flips[c] else u
            pairs.append((c * uly + u, d * uly + (mirror[group] if flips[d] else group)))
    return lax.ppermute(shard, ("ctx", "uly"), pairs)


def mirrored(x, flip, cores):
    rows, uly = x.shape[0], x.shape[1]
    split = x.reshape(rows, uly // cores, cores, x.shape[2])
    return jnp.where(flip, split[:, ::-1], split).reshape(x.shape)


def attention_kernel(
    meta_ref, q_ref, do_ref, k_ref, v_ref, qs_ref,
    dq_ref, dk_ref, dv_ref,
    m_s, l_s, acc_s, lse_s, delta_s, dq_s,
    *, groups, q_blocks, scale,
):
    T, TK, D = Q_BLOCK, K_BLOCK, HEAD_SIZE
    dk_ref[...] = jnp.zeros_like(dk_ref)
    dv_ref[...] = jnp.zeros_like(dv_ref)
    q_base = meta_ref[0]
    k_base = meta_ref[1]

    def tile_mask(q0, kb):
        q_pos = q_base + q0 + lax.broadcasted_iota(jnp.int32, (T, TK), 0)
        k_pos = k_base + kb * TK + lax.broadcasted_iota(jnp.int32, (T, TK), 1)
        start = qs_ref[pl.ds(q0, T), :]
        return (k_pos <= q_pos) & (k_pos >= start)

    def q_block(qb, carry):
        q0 = pl.multiple_of(qb * T, T)
        lo = meta_ref[2 + 2 * qb]
        hi = meta_ref[3 + 2 * qb]
        m_s[...] = jnp.full_like(m_s, NEG)
        l_s[...] = jnp.zeros_like(l_s)
        acc_s[...] = jnp.zeros_like(acc_s)

        def fwd(kb, c):
            k0 = pl.multiple_of(kb * TK, TK)
            k = k_ref[pl.ds(k0, TK), :]
            v = v_ref[pl.ds(k0, TK), :]
            mask = tile_mask(q0, kb)
            for h in range(groups):
                qh = q_ref[pl.ds(q0, T), pl.ds(h * D, D)]
                raw = lax.dot_general(
                    qh, k, (((1,), (1,)), ((), ())), preferred_element_type=jnp.float32
                ) * scale
                s = jnp.where(mask, raw, NEG)
                old_high = m_s[h]
                new_high = jnp.maximum(old_high, jnp.max(s, axis=1, keepdims=True))
                factor = jnp.exp(old_high - new_high)
                terms = jnp.where(mask, jnp.exp(s - new_high), 0.0)
                l_s[h] = l_s[h] * factor + jnp.sum(terms, axis=1, keepdims=True)
                acc_s[h] = acc_s[h] * factor + jnp.dot(
                    terms.astype(jnp.bfloat16), v, preferred_element_type=jnp.float32
                )
                m_s[h] = new_high
            return c

        lax.fori_loop(lo, hi, fwd, 0)
        for h in range(groups):
            total = l_s[h]
            lse_s[h] = m_s[h] + jnp.log(total)
            out = (acc_s[h] / total).astype(jnp.bfloat16).astype(jnp.float32)
            g = do_ref[pl.ds(q0, T), pl.ds(h * D, D)].astype(jnp.float32)
            delta_s[h] = jnp.sum(g * out, axis=1, keepdims=True)
        dq_s[...] = jnp.zeros_like(dq_s)

        def bwd(kb, c):
            k0 = pl.multiple_of(kb * TK, TK)
            k = k_ref[pl.ds(k0, TK), :]
            v = v_ref[pl.ds(k0, TK), :]
            mask = tile_mask(q0, kb)
            add_k = jnp.zeros((TK, D), jnp.float32)
            add_v = jnp.zeros((TK, D), jnp.float32)
            for h in range(groups):
                qh = q_ref[pl.ds(q0, T), pl.ds(h * D, D)]
                gh = do_ref[pl.ds(q0, T), pl.ds(h * D, D)]
                raw = lax.dot_general(
                    qh, k, (((1,), (1,)), ((), ())), preferred_element_type=jnp.float32
                ) * scale
                s = jnp.where(mask, raw, NEG)
                probs = jnp.where(mask, jnp.exp(s - lse_s[h]), 0.0)
                dprobs = lax.dot_general(
                    gh, v, (((1,), (1,)), ((), ())), preferred_element_type=jnp.float32
                )
                dscores = probs * (dprobs - delta_s[h])
                dq_s[h] = dq_s[h] + jnp.dot(
                    dscores.astype(jnp.bfloat16), k, preferred_element_type=jnp.float32
                )
                add_k = add_k + jnp.dot(
                    dscores.T.astype(jnp.bfloat16), qh, preferred_element_type=jnp.float32
                )
                add_v = add_v + jnp.dot(
                    probs.T.astype(jnp.bfloat16), gh, preferred_element_type=jnp.float32
                )
            dk_ref[pl.ds(k0, TK), :] = dk_ref[pl.ds(k0, TK), :] + add_k
            dv_ref[pl.ds(k0, TK), :] = dv_ref[pl.ds(k0, TK), :] + add_v
            return c

        lax.fori_loop(lo, hi, bwd, 0)
        for h in range(groups):
            dq_ref[pl.ds(q0, T), pl.ds(h * D, D)] = (scale * dq_s[h]).astype(dq_ref.dtype)
        return carry

    lax.fori_loop(0, q_blocks, q_block, 0)


def attend(meta, queries, gradient, key_window, value_window, q_start, groups, scale):
    rows = queries.shape[0]
    width = key_window.shape[0]
    q_blocks = rows // Q_BLOCK
    vmem = pltpu.MemorySpace.VMEM
    kernel = functools.partial(
        attention_kernel, groups=groups, q_blocks=q_blocks, scale=scale
    )
    return pl.pallas_call(
        kernel,
        out_shape=(
            jax.ShapeDtypeStruct(queries.shape, jnp.bfloat16),
            jax.ShapeDtypeStruct((width, HEAD_SIZE), jnp.float32),
            jax.ShapeDtypeStruct((width, HEAD_SIZE), jnp.float32),
        ),
        in_specs=[pl.BlockSpec(memory_space=pltpu.MemorySpace.SMEM)]
        + [pl.BlockSpec(memory_space=vmem)] * 5,
        out_specs=[pl.BlockSpec(memory_space=vmem)] * 3,
        scratch_shapes=[
            pltpu.VMEM((groups, Q_BLOCK, 1), jnp.float32),
            pltpu.VMEM((groups, Q_BLOCK, 1), jnp.float32),
            pltpu.VMEM((groups, Q_BLOCK, HEAD_SIZE), jnp.float32),
            pltpu.VMEM((groups, Q_BLOCK, 1), jnp.float32),
            pltpu.VMEM((groups, Q_BLOCK, 1), jnp.float32),
            pltpu.VMEM((groups, Q_BLOCK, HEAD_SIZE), jnp.float32),
        ],
        compiler_params=pltpu.CompilerParams(vmem_limit_bytes=48 * 1024 * 1024),
    )(meta, queries, gradient, key_window, value_window, q_start)


def on_device(queries, keys, values, output_gradient, doc_lengths, flips, cores):
    uly = lax.axis_size("uly")
    ctx_index = lax.axis_index("ctx")
    flip = jnp.asarray(flips)[ctx_index]
    tokens = queries.shape[0]
    q_cols = queries.shape[1] // uly
    kv_cols = keys.shape[1] // uly
    kv = jnp.concatenate(
        [keys.reshape(tokens, uly, kv_cols), values.reshape(tokens, uly, kv_cols)], axis=2
    )
    kv = lax.all_to_all(mirrored(kv, flip, cores), "uly", split_axis=1, concat_axis=0, tiled=True)
    rows = kv.shape[0]
    kv = kv.reshape(rows, 2 * kv_cols)
    window = [kv]
    for step in range(1, REACH + 1):
        window.append(from_behind(kv, step, flips, cores))
    packed = jnp.concatenate(
        [queries.reshape(tokens, uly, q_cols), output_gradient.reshape(tokens, uly, q_cols)],
        axis=2,
    )
    packed = mirrored(packed, flip, cores)
    packed = lax.all_to_all(packed, "uly", split_axis=1, concat_axis=0, tiled=True)
    packed = packed.reshape(rows, 2 * q_cols)
    queries = packed[:, :q_cols]
    gradient = packed[:, q_cols:]
    groups = q_cols // HEAD_SIZE
    softmax_scale = 1.0 / math.sqrt(HEAD_SIZE)

    window = jnp.concatenate(window[::-1], axis=0)
    key_window = window[:, :HEAD_SIZE]
    value_window = window[:, HEAD_SIZE:]

    q_base = ctx_index * rows
    k_base = (ctx_index - REACH) * rows
    q_pos = q_base + jnp.arange(rows, dtype=jnp.int32)
    ends = jnp.cumsum(doc_lengths)
    q_start = jnp.sum(
        jnp.where(ends[None, :] <= q_pos[:, None], doc_lengths[None, :], 0), axis=1
    ).astype(jnp.int32)
    first_rows = jnp.arange(0, rows, Q_BLOCK, dtype=jnp.int32)
    lo = jnp.maximum((q_start[first_rows] - k_base) // K_BLOCK, 0)
    hi = (q_base + first_rows + Q_BLOCK - 1 - k_base) // K_BLOCK + 1
    meta = jnp.concatenate(
        [jnp.stack([q_base, k_base]).astype(jnp.int32), jnp.stack([lo, hi], axis=1).reshape(-1)]
    ).astype(jnp.int32)

    dq, dk_window, dv_window = attend(
        meta, queries, gradient, key_window, value_window, q_start[:, None], groups, softmax_scale
    )
    partials = jnp.concatenate([dk_window, dv_window], axis=1)
    returned = [
        from_behind(
            partials[(REACH - step) * rows : (REACH - step + 1) * rows].astype(jnp.bfloat16),
            -step,
            flips,
            cores,
        )
        for step in range(1, REACH + 1)
    ]
    out_q = lax.all_to_all(dq, "uly", split_axis=0, concat_axis=1, tiled=True)
    out_q, returned = lax.optimization_barrier((out_q, returned))
    out_q = mirrored(out_q.reshape(out_q.shape[0], uly, q_cols), flip, cores)
    total = partials[REACH * rows :]
    for piece in returned:
        total = total + piece.astype(jnp.float32)
    out_k = (softmax_scale * total[:, :HEAD_SIZE]).astype(jnp.bfloat16)
    out_v = total[:, HEAD_SIZE:].astype(jnp.bfloat16)
    out_kv = lax.all_to_all(
        jnp.concatenate([out_k, out_v], axis=1), "uly", split_axis=0, concat_axis=1, tiled=True
    )
    out_kv = mirrored(out_kv.reshape(out_kv.shape[0], uly, 2 * kv_cols), flip, cores)
    return (
        out_q.reshape(out_q.shape[0], uly * q_cols),
        out_kv[:, :, :kv_cols].reshape(out_kv.shape[0], uly * kv_cols),
        out_kv[:, :, kv_cols:].reshape(out_kv.shape[0], uly * kv_cols),
    )


def layout_of(mesh):
    devices = mesh.devices
    cores = len({getattr(d, "core_on_chip", 0) for d in devices.flat})
    run = devices.shape[1] // cores
    coords = [getattr(devices[c, 0], "coords", None) for c in range(devices.shape[0])]
    if any(xyz is None for xyz in coords):
        return (False,) * devices.shape[0], cores
    return tuple(bool((xyz[2] // run) % 2) for xyz in coords), cores


def solution(mesh):
    flips, cores = layout_of(mesh)
    return jax.shard_map(
        functools.partial(on_device, flips=flips, cores=cores),
        mesh=mesh,
        in_specs=(
            P(("ctx", "uly"), None),
            P(("ctx", "uly"), None),
            P(("ctx", "uly"), None),
            P(("ctx", "uly"), None),
            P(),
        ),
        out_specs=(P(("ctx", "uly"), None), P(("ctx", "uly"), None), P(("ctx", "uly"), None)),
        check_vma=False,
    )
```

```python
import functools
import math

import jax
import jax.numpy as jnp
from jax import lax
from jax.experimental import pallas as pl
from jax.experimental.pallas import tpu as pltpu
from jax.sharding import PartitionSpec as P

HEAD_SIZE = 128
REACH = 3
Q_BLOCK = 512
K_BLOCK = 512

NEG = -1e30


def mirror_of(uly, cores):
    run = uly // cores
    return [(run - 1 - u // cores) * cores + u % cores for u in range(uly)]


def from_behind(shard, by, flips, cores):
    ctx = lax.axis_size("ctx")
    uly = lax.axis_size("uly")
    mirror = mirror_of(uly, cores)
    pairs = []
    for c in range(ctx):
        d = c + by
        if not 0 <= d < ctx:
            continue
        for u in range(uly):
            group = mirror[u] if flips[c] else u
            pairs.append((c * uly + u, d * uly + (mirror[group] if flips[d] else group)))
    return lax.ppermute(shard, ("ctx", "uly"), pairs)


def mirrored(x, flip, cores):
    rows, uly = x.shape[0], x.shape[1]
    split = x.reshape(rows, uly // cores, cores, x.shape[2])
    return jnp.where(flip, split[:, ::-1], split).reshape(x.shape)


def attention_kernel(
    meta_ref, q_ref, do_ref, k_ref, v_ref, qs_ref, qsr_ref,
    dq_ref, dk_ref, dv_ref,
    m_s, l_s, acc_s, lse_s, delta_s, dq_s,
    *, groups, q_blocks, scale,
):
    T, TK, D = Q_BLOCK, K_BLOCK, HEAD_SIZE
    nt = (((1,), (1,)), ((), ()))
    dk_ref[...] = jnp.zeros_like(dk_ref)
    dv_ref[...] = jnp.zeros_like(dv_ref)
    q_base = meta_ref[0]
    k_base = meta_ref[1]

    def q_block(qb, carry):
        q0 = pl.multiple_of(qb * T, T)
        lo = meta_ref[2 + 2 * qb]
        hi = meta_ref[3 + 2 * qb]
        m_s[...] = jnp.full_like(m_s, NEG)
        l_s[...] = jnp.zeros_like(l_s)
        acc_s[...] = jnp.zeros_like(acc_s)

        def fwd(kb, c):
            k0 = pl.multiple_of(kb * TK, TK)
            k = k_ref[pl.ds(k0, TK), :]
            v_t = v_ref[pl.ds(k0, TK), :].astype(jnp.float32).T.astype(jnp.bfloat16)
            k_pos = k_base + k0 + lax.broadcasted_iota(jnp.int32, (TK, T), 0)
            q_pos = q_base + q0 + lax.broadcasted_iota(jnp.int32, (TK, T), 1)
            start = qsr_ref[:, pl.ds(q0, T)]
            mask = (k_pos <= q_pos) & (k_pos >= start)
            for h in range(groups):
                qh = q_ref[pl.ds(q0, T), pl.ds(h * D, D)]
                raw = lax.dot_general(k, qh, nt, preferred_element_type=jnp.float32) * scale
                s = jnp.where(mask, raw, NEG)
                old_high = m_s[h]
                new_high = jnp.maximum(old_high, jnp.max(s, axis=0, keepdims=True))
                factor = jnp.exp(old_high - new_high)
                terms = jnp.exp(s - new_high)
                l_s[h] = l_s[h] * factor + jnp.sum(terms, axis=0, keepdims=True)
                acc_s[h] = acc_s[h] * factor + jnp.dot(
                    v_t, terms.astype(jnp.bfloat16), preferred_element_type=jnp.float32
                )
                m_s[h] = new_high
            return c

        lax.fori_loop(lo, hi, fwd, 0)
        for h in range(groups):
            total = l_s[h]
            lse_s[h] = m_s[h] + jnp.log(total)
            out = (acc_s[h] / total).astype(jnp.bfloat16).astype(jnp.float32)
            g = do_ref[pl.ds(q0, T), pl.ds(h * D, D)].astype(jnp.float32).T
            delta_s[h] = jnp.sum(g * out, axis=0, keepdims=True)
        dq_s[...] = jnp.zeros_like(dq_s)

        def bwd(kb, c):
            k0 = pl.multiple_of(kb * TK, TK)
            k = k_ref[pl.ds(k0, TK), :]
            v = v_ref[pl.ds(k0, TK), :]
            k_t = k.astype(jnp.float32).T.astype(jnp.bfloat16)
            k_pos = k_base + k0 + lax.broadcasted_iota(jnp.int32, (TK, T), 0)
            q_pos = q_base + q0 + lax.broadcasted_iota(jnp.int32, (TK, T), 1)
            start = qsr_ref[:, pl.ds(q0, T)]
            mask = (k_pos <= q_pos) & (k_pos >= start)
            add_k = jnp.zeros((TK, D), jnp.float32)
            add_v = jnp.zeros((TK, D), jnp.float32)
            for h in range(groups):
                qh = q_ref[pl.ds(q0, T), pl.ds(h * D, D)]
                gh = do_ref[pl.ds(q0, T), pl.ds(h * D, D)]
                raw = lax.dot_general(k, qh, nt, preferred_element_type=jnp.float32) * scale
                probs = jnp.where(mask, jnp.exp(raw - lse_s[h]), 0.0)
                dprobs = lax.dot_general(v, gh, nt, preferred_element_type=jnp.float32)
                dscores = (probs * (dprobs - delta_s[h])).astype(jnp.bfloat16)
                add_v = add_v + jnp.dot(
                    probs.astype(jnp.bfloat16), gh, preferred_element_type=jnp.float32
                )
                add_k = add_k + jnp.dot(dscores, qh, preferred_element_type=jnp.float32)
                dq_s[h] = dq_s[h] + jnp.dot(k_t, dscores, preferred_element_type=jnp.float32)
            dk_ref[pl.ds(k0, TK), :] = dk_ref[pl.ds(k0, TK), :] + add_k
            dv_ref[pl.ds(k0, TK), :] = dv_ref[pl.ds(k0, TK), :] + add_v
            return c

        lax.fori_loop(lo, hi, bwd, 0)
        for h in range(groups):
            dq_ref[pl.ds(q0, T), pl.ds(h * D, D)] = (scale * dq_s[h].T).astype(dq_ref.dtype)
        return carry

    lax.fori_loop(0, q_blocks, q_block, 0)


def attend(meta, queries, gradient, key_window, value_window, q_start, groups, scale):
    rows = queries.shape[0]
    width = key_window.shape[0]
    q_blocks = rows // Q_BLOCK
    vmem = pltpu.MemorySpace.VMEM
    kernel = functools.partial(
        attention_kernel, groups=groups, q_blocks=q_blocks, scale=scale
    )
    return pl.pallas_call(
        kernel,
        out_shape=(
            jax.ShapeDtypeStruct(queries.shape, jnp.bfloat16),
            jax.ShapeDtypeStruct((width, HEAD_SIZE), jnp.float32),
            jax.ShapeDtypeStruct((width, HEAD_SIZE), jnp.float32),
        ),
        in_specs=[pl.BlockSpec(memory_space=pltpu.MemorySpace.SMEM)]
        + [pl.BlockSpec(memory_space=vmem)] * 6,
        out_specs=[pl.BlockSpec(memory_space=vmem)] * 3,
        scratch_shapes=[
            pltpu.VMEM((groups, 1, Q_BLOCK), jnp.float32),
            pltpu.VMEM((groups, 1, Q_BLOCK), jnp.float32),
            pltpu.VMEM((groups, HEAD_SIZE, Q_BLOCK), jnp.float32),
            pltpu.VMEM((groups, 1, Q_BLOCK), jnp.float32),
            pltpu.VMEM((groups, 1, Q_BLOCK), jnp.float32),
            pltpu.VMEM((groups, HEAD_SIZE, Q_BLOCK), jnp.float32),
        ],
        compiler_params=pltpu.CompilerParams(vmem_limit_bytes=48 * 1024 * 1024),
    )(meta, queries, gradient, key_window, value_window, q_start, q_start.reshape(1, rows))


def on_device(queries, keys, values, output_gradient, doc_lengths, flips, cores):
    uly = lax.axis_size("uly")
    ctx_index = lax.axis_index("ctx")
    flip = jnp.asarray(flips)[ctx_index]
    tokens = queries.shape[0]
    q_cols = queries.shape[1] // uly
    kv_cols = keys.shape[1] // uly
    kv = jnp.concatenate(
        [keys.reshape(tokens, uly, kv_cols), values.reshape(tokens, uly, kv_cols)], axis=2
    )
    kv = lax.all_to_all(mirrored(kv, flip, cores), "uly", split_axis=1, concat_axis=0, tiled=True)
    rows = kv.shape[0]
    kv = kv.reshape(rows, 2 * kv_cols)
    window = [kv]
    for step in range(1, REACH + 1):
        window.append(from_behind(kv, step, flips, cores))
    packed = jnp.concatenate(
        [queries.reshape(tokens, uly, q_cols), output_gradient.reshape(tokens, uly, q_cols)],
        axis=2,
    )
    packed = mirrored(packed, flip, cores)
    packed = lax.all_to_all(packed, "uly", split_axis=1, concat_axis=0, tiled=True)
    packed = packed.reshape(rows, 2 * q_cols)
    queries = packed[:, :q_cols]
    gradient = packed[:, q_cols:]
    groups = q_cols // HEAD_SIZE
    softmax_scale = 1.0 / math.sqrt(HEAD_SIZE)

    window = jnp.concatenate(window[::-1], axis=0)
    key_window = window[:, :HEAD_SIZE]
    value_window = window[:, HEAD_SIZE:]

    q_base = ctx_index * rows
    k_base = (ctx_index - REACH) * rows
    q_pos = q_base + jnp.arange(rows, dtype=jnp.int32)
    ends = jnp.cumsum(doc_lengths)
    q_start = jnp.sum(
        jnp.where(ends[None, :] <= q_pos[:, None], doc_lengths[None, :], 0), axis=1
    ).astype(jnp.int32)
    first_rows = jnp.arange(0, rows, Q_BLOCK, dtype=jnp.int32)
    lo = jnp.maximum((q_start[first_rows] - k_base) // K_BLOCK, 0)
    hi = (q_base + first_rows + Q_BLOCK - 1 - k_base) // K_BLOCK + 1
    meta = jnp.concatenate(
        [jnp.stack([q_base, k_base]).astype(jnp.int32), jnp.stack([lo, hi], axis=1).reshape(-1)]
    ).astype(jnp.int32)

    dq, dk_window, dv_window = attend(
        meta, queries, gradient, key_window, value_window, q_start[:, None], groups, softmax_scale
    )
    partials = jnp.concatenate([dk_window, dv_window], axis=1)
    returned = [
        from_behind(
            partials[(REACH - step) * rows : (REACH - step + 1) * rows].astype(jnp.bfloat16),
            -step,
            flips,
            cores,
        )
        for step in range(1, REACH + 1)
    ]
    out_q = lax.all_to_all(dq, "uly", split_axis=0, concat_axis=1, tiled=True)
    out_q, returned = lax.optimization_barrier((out_q, returned))
    out_q = mirrored(out_q.reshape(out_q.shape[0], uly, q_cols), flip, cores)
    total = partials[REACH * rows :]
    for piece in returned:
        total = total + piece.astype(jnp.float32)
    out_k = (softmax_scale * total[:, :HEAD_SIZE]).astype(jnp.bfloat16)
    out_v = total[:, HEAD_SIZE:].astype(jnp.bfloat16)
    out_kv = lax.all_to_all(
        jnp.concatenate([out_k, out_v], axis=1), "uly", split_axis=0, concat_axis=1, tiled=True
    )
    out_kv = mirrored(out_kv.reshape(out_kv.shape[0], uly, 2 * kv_cols), flip, cores)
    return (
        out_q.reshape(out_q.shape[0], uly * q_cols),
        out_kv[:, :, :kv_cols].reshape(out_kv.shape[0], uly * kv_cols),
        out_kv[:, :, kv_cols:].reshape(out_kv.shape[0], uly * kv_cols),
    )


def layout_of(mesh):
    devices = mesh.devices
    cores = len({getattr(d, "core_on_chip", 0) for d in devices.flat})
    run = devices.shape[1] // cores
    coords = [getattr(devices[c, 0], "coords", None) for c in range(devices.shape[0])]
    if any(xyz is None for xyz in coords):
        return (False,) * devices.shape[0], cores
    return tuple(bool((xyz[2] // run) % 2) for xyz in coords), cores


def solution(mesh):
    flips, cores = layout_of(mesh)
    return jax.shard_map(
        functools.partial(on_device, flips=flips, cores=cores),
        mesh=mesh,
        in_specs=(
            P(("ctx", "uly"), None),
            P(("ctx", "uly"), None),
            P(("ctx", "uly"), None),
            P(("ctx", "uly"), None),
            P(),
        ),
        out_specs=(P(("ctx", "uly"), None), P(("ctx", "uly"), None), P(("ctx", "uly"), None)),
        check_vma=False,
    )
```

```python
import functools
import math

import jax
import jax.numpy as jnp
from jax import lax
from jax.experimental import pallas as pl
from jax.experimental.pallas import tpu as pltpu
from jax.sharding import PartitionSpec as P

HEAD_SIZE = 128
REACH = 3
Q_BLOCK = 512
K_BLOCK = 512

NEG = -1e30


def mirror_of(uly, cores):
    run = uly // cores
    return [(run - 1 - u // cores) * cores + u % cores for u in range(uly)]


def from_behind(shard, by, flips, cores):
    ctx = lax.axis_size("ctx")
    uly = lax.axis_size("uly")
    mirror = mirror_of(uly, cores)
    pairs = []
    for c in range(ctx):
        d = c + by
        if not 0 <= d < ctx:
            continue
        for u in range(uly):
            group = mirror[u] if flips[c] else u
            pairs.append((c * uly + u, d * uly + (mirror[group] if flips[d] else group)))
    return lax.ppermute(shard, ("ctx", "uly"), pairs)


def mirrored(x, flip, cores):
    rows, uly = x.shape[0], x.shape[1]
    split = x.reshape(rows, uly // cores, cores, x.shape[2])
    return jnp.where(flip, split[:, ::-1], split).reshape(x.shape)


def attention_kernel(
    meta_ref, q_ref, do_ref, k_ref, v_ref, qs_ref, qsr_ref,
    dq_ref, dkv_ref,
    m_s, l_s, acc_s, lse_s, delta_s, dq_s,
    *, groups, q_blocks, scale,
):
    T, TK, D = Q_BLOCK, K_BLOCK, HEAD_SIZE
    nt = (((1,), (1,)), ((), ()))
    dkv_ref[...] = jnp.zeros_like(dkv_ref)
    q_base = meta_ref[0]
    k_base = meta_ref[1]

    def q_block(qb, carry):
        q0 = pl.multiple_of(qb * T, T)
        lo = meta_ref[2 + 3 * qb]
        hi = meta_ref[3 + 3 * qb]
        last_start = meta_ref[4 + 3 * qb]
        m_s[...] = jnp.full_like(m_s, NEG)
        l_s[...] = jnp.zeros_like(l_s)
        acc_s[...] = jnp.zeros_like(acc_s)

        def tile_mask(k0):
            k_pos = k_base + k0 + lax.broadcasted_iota(jnp.int32, (TK, T), 0)
            q_pos = q_base + q0 + lax.broadcasted_iota(jnp.int32, (TK, T), 1)
            start = qsr_ref[:, pl.ds(q0, T)]
            return (k_pos <= q_pos) & (k_pos >= start)

        def is_full(k0):
            return (k_base + k0 + TK - 1 <= q_base + q0) & (k_base + k0 >= last_start)

        def fwd_tile(k0, masked):
            k = k_ref[pl.ds(k0, TK), :]
            v_t = v_ref[pl.ds(k0, TK), :].astype(jnp.float32).T.astype(jnp.bfloat16)
            mask = tile_mask(k0) if masked else None
            for h in range(groups):
                qh = q_ref[pl.ds(q0, T), pl.ds(h * D, D)]
                raw = lax.dot_general(k, qh, nt, preferred_element_type=jnp.float32) * scale
                s = jnp.where(mask, raw, NEG) if masked else raw
                old_high = m_s[h]
                new_high = jnp.maximum(old_high, jnp.max(s, axis=0, keepdims=True))
                factor = jnp.exp(old_high - new_high)
                terms = jnp.exp(s - new_high)
                l_s[h] = l_s[h] * factor + jnp.sum(terms, axis=0, keepdims=True)
                acc_s[h] = acc_s[h] * factor + jnp.dot(
                    v_t, terms.astype(jnp.bfloat16), preferred_element_type=jnp.float32
                )
                m_s[h] = new_high

        def fwd(kb, c):
            k0 = pl.multiple_of(kb * TK, TK)
            full = is_full(k0)
            pl.when(full)(lambda: fwd_tile(k0, False))
            pl.when(jnp.logical_not(full))(lambda: fwd_tile(k0, True))
            return c

        lax.fori_loop(lo, hi, fwd, 0)
        for h in range(groups):
            total = l_s[h]
            lse_s[h] = m_s[h] + jnp.log(total)
            out = (acc_s[h] / total).astype(jnp.bfloat16).astype(jnp.float32)
            g = do_ref[pl.ds(q0, T), pl.ds(h * D, D)].astype(jnp.float32).T
            delta_s[h] = jnp.sum(g * out, axis=0, keepdims=True)
        dq_s[...] = jnp.zeros_like(dq_s)

        def bwd_tile(k0, masked):
            k = k_ref[pl.ds(k0, TK), :]
            v = v_ref[pl.ds(k0, TK), :]
            k_t = k.astype(jnp.float32).T.astype(jnp.bfloat16)
            mask = tile_mask(k0) if masked else None
            add_k = jnp.zeros((TK, D), jnp.float32)
            add_v = jnp.zeros((TK, D), jnp.float32)
            for h in range(groups):
                qh = q_ref[pl.ds(q0, T), pl.ds(h * D, D)]
                gh = do_ref[pl.ds(q0, T), pl.ds(h * D, D)]
                raw = lax.dot_general(k, qh, nt, preferred_element_type=jnp.float32) * scale
                probs = jnp.exp(raw - lse_s[h])
                if masked:
                    probs = jnp.where(mask, probs, 0.0)
                dprobs = lax.dot_general(v, gh, nt, preferred_element_type=jnp.float32)
                dscores = (probs * (dprobs - delta_s[h])).astype(jnp.bfloat16)
                add_v = add_v + jnp.dot(
                    probs.astype(jnp.bfloat16), gh, preferred_element_type=jnp.float32
                )
                add_k = add_k + jnp.dot(dscores, qh, preferred_element_type=jnp.float32)
                dq_s[h] = dq_s[h] + jnp.dot(k_t, dscores, preferred_element_type=jnp.float32)
            dkv_ref[pl.ds(k0, TK), pl.ds(0, D)] = dkv_ref[pl.ds(k0, TK), pl.ds(0, D)] + add_k
            dkv_ref[pl.ds(k0, TK), pl.ds(D, D)] = dkv_ref[pl.ds(k0, TK), pl.ds(D, D)] + add_v

        def bwd(kb, c):
            k0 = pl.multiple_of(kb * TK, TK)
            full = is_full(k0)
            pl.when(full)(lambda: bwd_tile(k0, False))
            pl.when(jnp.logical_not(full))(lambda: bwd_tile(k0, True))
            return c

        lax.fori_loop(lo, hi, bwd, 0)
        for h in range(groups):
            dq_ref[pl.ds(q0, T), pl.ds(h * D, D)] = (scale * dq_s[h].T).astype(dq_ref.dtype)
        return carry

    lax.fori_loop(0, q_blocks, q_block, 0)


def attend(meta, queries, gradient, key_window, value_window, q_start, groups, scale):
    rows = queries.shape[0]
    width = key_window.shape[0]
    q_blocks = rows // Q_BLOCK
    vmem = pltpu.MemorySpace.VMEM
    kernel = functools.partial(
        attention_kernel, groups=groups, q_blocks=q_blocks, scale=scale
    )
    return pl.pallas_call(
        kernel,
        out_shape=(
            jax.ShapeDtypeStruct(queries.shape, jnp.bfloat16),
            jax.ShapeDtypeStruct((width, 2 * HEAD_SIZE), jnp.float32),
        ),
        in_specs=[pl.BlockSpec(memory_space=pltpu.MemorySpace.SMEM)]
        + [pl.BlockSpec(memory_space=vmem)] * 6,
        out_specs=[pl.BlockSpec(memory_space=vmem)] * 2,
        scratch_shapes=[
            pltpu.VMEM((groups, 1, Q_BLOCK), jnp.float32),
            pltpu.VMEM((groups, 1, Q_BLOCK), jnp.float32),
            pltpu.VMEM((groups, HEAD_SIZE, Q_BLOCK), jnp.float32),
            pltpu.VMEM((groups, 1, Q_BLOCK), jnp.float32),
            pltpu.VMEM((groups, 1, Q_BLOCK), jnp.float32),
            pltpu.VMEM((groups, HEAD_SIZE, Q_BLOCK), jnp.float32),
        ],
        compiler_params=pltpu.CompilerParams(vmem_limit_bytes=48 * 1024 * 1024),
    )(meta, queries, gradient, key_window, value_window, q_start, q_start.reshape(1, rows))


def on_device(queries, keys, values, output_gradient, doc_lengths, flips, cores):
    uly = lax.axis_size("uly")
    ctx_index = lax.axis_index("ctx")
    flip = jnp.asarray(flips)[ctx_index]
    tokens = queries.shape[0]
    q_cols = queries.shape[1] // uly
    kv_cols = keys.shape[1] // uly
    kv = jnp.concatenate(
        [keys.reshape(tokens, uly, kv_cols), values.reshape(tokens, uly, kv_cols)], axis=2
    )
    kv = lax.all_to_all(mirrored(kv, flip, cores), "uly", split_axis=1, concat_axis=0, tiled=True)
    rows = kv.shape[0]
    kv = kv.reshape(rows, 2 * kv_cols)
    window = [kv]
    for step in range(1, REACH + 1):
        window.append(from_behind(kv, step, flips, cores))
    packed = jnp.concatenate(
        [queries.reshape(tokens, uly, q_cols), output_gradient.reshape(tokens, uly, q_cols)],
        axis=2,
    )
    packed = mirrored(packed, flip, cores)
    packed = lax.all_to_all(packed, "uly", split_axis=1, concat_axis=0, tiled=True)
    packed = packed.reshape(rows, 2 * q_cols)
    queries = packed[:, :q_cols]
    gradient = packed[:, q_cols:]
    groups = q_cols // HEAD_SIZE
    softmax_scale = 1.0 / math.sqrt(HEAD_SIZE)

    window = jnp.concatenate(window[::-1], axis=0)
    key_window = window[:, :HEAD_SIZE]
    value_window = window[:, HEAD_SIZE:]

    q_base = ctx_index * rows
    k_base = (ctx_index - REACH) * rows
    q_pos = q_base + jnp.arange(rows, dtype=jnp.int32)
    ends = jnp.cumsum(doc_lengths)
    q_start = jnp.sum(
        jnp.where(ends[None, :] <= q_pos[:, None], doc_lengths[None, :], 0), axis=1
    ).astype(jnp.int32)
    first_rows = jnp.arange(0, rows, Q_BLOCK, dtype=jnp.int32)
    lo = jnp.maximum((q_start[first_rows] - k_base) // K_BLOCK, 0)
    hi = (q_base + first_rows + Q_BLOCK - 1 - k_base) // K_BLOCK + 1
    meta = jnp.concatenate(
        [jnp.stack([q_base, k_base]).astype(jnp.int32), jnp.stack([lo, hi, q_start[first_rows + Q_BLOCK - 1]], axis=1).reshape(-1)]
    ).astype(jnp.int32)

    dq, partials = attend(
        meta, queries, gradient, key_window, value_window, q_start[:, None], groups, softmax_scale
    )
    returned = [
        from_behind(
            partials[(REACH - step) * rows : (REACH - step + 1) * rows].astype(jnp.bfloat16),
            -step,
            flips,
            cores,
        )
        for step in range(1, REACH + 1)
    ]
    out_q = lax.all_to_all(dq, "uly", split_axis=0, concat_axis=1, tiled=True)
    out_q, returned = lax.optimization_barrier((out_q, returned))
    out_q = mirrored(out_q.reshape(out_q.shape[0], uly, q_cols), flip, cores)
    total = partials[REACH * rows :]
    for piece in returned:
        total = total + piece.astype(jnp.float32)
    out_k = (softmax_scale * total[:, :HEAD_SIZE]).astype(jnp.bfloat16)
    out_v = total[:, HEAD_SIZE:].astype(jnp.bfloat16)
    out_kv = lax.all_to_all(
        jnp.concatenate([out_k, out_v], axis=1), "uly", split_axis=0, concat_axis=1, tiled=True
    )
    out_kv = mirrored(out_kv.reshape(out_kv.shape[0], uly, 2 * kv_cols), flip, cores)
    return (
        out_q.reshape(out_q.shape[0], uly * q_cols),
        out_kv[:, :, :kv_cols].reshape(out_kv.shape[0], uly * kv_cols),
        out_kv[:, :, kv_cols:].reshape(out_kv.shape[0], uly * kv_cols),
    )


def layout_of(mesh):
    devices = mesh.devices
    cores = len({getattr(d, "core_on_chip", 0) for d in devices.flat})
    run = devices.shape[1] // cores
    coords = [getattr(devices[c, 0], "coords", None) for c in range(devices.shape[0])]
    if any(xyz is None for xyz in coords):
        return (False,) * devices.shape[0], cores
    return tuple(bool((xyz[2] // run) % 2) for xyz in coords), cores


def solution(mesh):
    flips, cores = layout_of(mesh)
    return jax.shard_map(
        functools.partial(on_device, flips=flips, cores=cores),
        mesh=mesh,
        in_specs=(
            P(("ctx", "uly"), None),
            P(("ctx", "uly"), None),
            P(("ctx", "uly"), None),
            P(("ctx", "uly"), None),
            P(),
        ),
        out_specs=(P(("ctx", "uly"), None), P(("ctx", "uly"), None), P(("ctx", "uly"), None)),
        check_vma=False,
    )
```

```python
import functools
import math

import jax
import jax.numpy as jnp
from jax import lax
from jax.experimental import pallas as pl
from jax.experimental.pallas import tpu as pltpu
from jax.sharding import PartitionSpec as P

HEAD_SIZE = 128
REACH = 3
Q_BLOCK = 512
K_BLOCK = 512

NEG = -1e30


def mirror_of(uly, cores):
    run = uly // cores
    return [(run - 1 - u // cores) * cores + u % cores for u in range(uly)]


def from_behind(shard, by, flips, cores):
    ctx = lax.axis_size("ctx")
    uly = lax.axis_size("uly")
    mirror = mirror_of(uly, cores)
    pairs = []
    for c in range(ctx):
        d = c + by
        if not 0 <= d < ctx:
            continue
        for u in range(uly):
            group = mirror[u] if flips[c] else u
            pairs.append((c * uly + u, d * uly + (mirror[group] if flips[d] else group)))
    return lax.ppermute(shard, ("ctx", "uly"), pairs)


def mirrored(x, flip, cores):
    rows, uly = x.shape[0], x.shape[1]
    split = x.reshape(rows, uly // cores, cores, x.shape[2])
    return jnp.where(flip, split[:, ::-1], split).reshape(x.shape)


def attention_kernel(
    meta_ref, q_ref, do_ref, k_ref, v_ref, qs_ref, qsr_ref,
    dq_ref, dk_ref, dv_ref,
    m_s, l_s, acc_s, lse_s, delta_s, dq_s,
    *, groups, q_blocks, scale,
):
    T, TK, D = Q_BLOCK, K_BLOCK, HEAD_SIZE
    nt = (((1,), (1,)), ((), ()))
    dk_ref[...] = jnp.zeros_like(dk_ref)
    dv_ref[...] = jnp.zeros_like(dv_ref)
    q_base = meta_ref[0]
    k_base = meta_ref[1]

    def q_block(qb, carry):
        q0 = pl.multiple_of(qb * T, T)
        lo = meta_ref[2 + 2 * qb]
        hi = meta_ref[3 + 2 * qb]
        m_s[...] = jnp.full_like(m_s, NEG)
        l_s[...] = jnp.zeros_like(l_s)
        acc_s[...] = jnp.zeros_like(acc_s)

        def fwd(kb, c):
            k0 = pl.multiple_of(kb * TK, TK)
            k = k_ref[pl.ds(k0, TK), :]
            v_t = v_ref[pl.ds(k0, TK), :].astype(jnp.float32).T.astype(jnp.bfloat16)
            k_pos = k_base + k0 + lax.broadcasted_iota(jnp.int32, (TK, T), 0)
            q_pos = q_base + q0 + lax.broadcasted_iota(jnp.int32, (TK, T), 1)
            start = qsr_ref[:, pl.ds(q0, T)]
            mask = (k_pos <= q_pos) & (k_pos >= start)
            for h in range(groups):
                qh = q_ref[pl.ds(q0, T), pl.ds(h * D, D)]
                raw = lax.dot_general(k, qh, nt, preferred_element_type=jnp.float32) * scale
                s = jnp.where(mask, raw, NEG)
                old_high = m_s[h]
                new_high = jnp.maximum(old_high, jnp.max(s, axis=0, keepdims=True))
                factor = jnp.exp(old_high - new_high)
                terms = jnp.exp(s - new_high)
                l_s[h] = l_s[h] * factor + jnp.sum(terms, axis=0, keepdims=True)
                acc_s[h] = acc_s[h] * factor + jnp.dot(
                    v_t, terms.astype(jnp.bfloat16), preferred_element_type=jnp.float32
                )
                m_s[h] = new_high
            return c

        lax.fori_loop(lo, hi, fwd, 0)
        for h in range(groups):
            total = l_s[h]
            lse_s[h] = m_s[h] + jnp.log(total)
            out = (acc_s[h] / total).astype(jnp.bfloat16).astype(jnp.float32)
            g = do_ref[pl.ds(q0, T), pl.ds(h * D, D)].astype(jnp.float32).T
            delta_s[h] = jnp.sum(g * out, axis=0, keepdims=True)
        dq_s[...] = jnp.zeros_like(dq_s)

        def bwd(kb, c):
            k0 = pl.multiple_of(kb * TK, TK)
            k = k_ref[pl.ds(k0, TK), :]
            v = v_ref[pl.ds(k0, TK), :]
            k_t = k.astype(jnp.float32).T.astype(jnp.bfloat16)
            k_pos = k_base + k0 + lax.broadcasted_iota(jnp.int32, (TK, T), 0)
            q_pos = q_base + q0 + lax.broadcasted_iota(jnp.int32, (TK, T), 1)
            start = qsr_ref[:, pl.ds(q0, T)]
            mask = (k_pos <= q_pos) & (k_pos >= start)
            add_k = jnp.zeros((TK, D), jnp.float32)
            add_v = jnp.zeros((TK, D), jnp.float32)
            for h in range(groups):
                qh = q_ref[pl.ds(q0, T), pl.ds(h * D, D)]
                gh = do_ref[pl.ds(q0, T), pl.ds(h * D, D)]
                raw = lax.dot_general(k, qh, nt, preferred_element_type=jnp.float32) * scale
                probs = jnp.where(mask, jnp.exp(raw - lse_s[h]), 0.0)
                dprobs = lax.dot_general(v, gh, nt, preferred_element_type=jnp.float32)
                dscores = (probs * (dprobs - delta_s[h])).astype(jnp.bfloat16)
                add_v = add_v + jnp.dot(
                    probs.astype(jnp.bfloat16), gh, preferred_element_type=jnp.float32
                )
                add_k = add_k + jnp.dot(dscores, qh, preferred_element_type=jnp.float32)
                dq_s[h] = dq_s[h] + jnp.dot(k_t, dscores, preferred_element_type=jnp.float32)
            dk_ref[pl.ds(k0, TK), :] = dk_ref[pl.ds(k0, TK), :] + add_k
            dv_ref[pl.ds(k0, TK), :] = dv_ref[pl.ds(k0, TK), :] + add_v
            return c

        lax.fori_loop(lo, hi, bwd, 0)
        for h in range(groups):
            dq_ref[pl.ds(q0, T), pl.ds(h * D, D)] = (scale * dq_s[h].T).astype(dq_ref.dtype)
        return carry

    lax.fori_loop(0, q_blocks, q_block, 0)


def attend(meta, queries, gradient, key_window, value_window, q_start, groups, scale):
    rows = queries.shape[0]
    width = key_window.shape[0]
    q_blocks = rows // Q_BLOCK
    vmem = pltpu.MemorySpace.VMEM
    kernel = functools.partial(
        attention_kernel, groups=groups, q_blocks=q_blocks, scale=scale
    )
    return pl.pallas_call(
        kernel,
        out_shape=(
            jax.ShapeDtypeStruct(queries.shape, jnp.bfloat16),
            jax.ShapeDtypeStruct((width, HEAD_SIZE), jnp.float32),
            jax.ShapeDtypeStruct((width, HEAD_SIZE), jnp.float32),
        ),
        in_specs=[pl.BlockSpec(memory_space=pltpu.MemorySpace.SMEM)]
        + [pl.BlockSpec(memory_space=vmem)] * 6,
        out_specs=[pl.BlockSpec(memory_space=vmem)] * 3,
        scratch_shapes=[
            pltpu.VMEM((groups, 1, Q_BLOCK), jnp.float32),
            pltpu.VMEM((groups, 1, Q_BLOCK), jnp.float32),
            pltpu.VMEM((groups, HEAD_SIZE, Q_BLOCK), jnp.float32),
            pltpu.VMEM((groups, 1, Q_BLOCK), jnp.float32),
            pltpu.VMEM((groups, 1, Q_BLOCK), jnp.float32),
            pltpu.VMEM((groups, HEAD_SIZE, Q_BLOCK), jnp.float32),
        ],
        compiler_params=pltpu.CompilerParams(vmem_limit_bytes=48 * 1024 * 1024),
    )(meta, queries, gradient, key_window, value_window, q_start, q_start.reshape(1, rows))


def on_device(queries, keys, values, output_gradient, doc_lengths, flips, cores):
    uly = lax.axis_size("uly")
    ctx_index = lax.axis_index("ctx")
    flip = jnp.asarray(flips)[ctx_index]
    tokens = queries.shape[0]
    q_cols = queries.shape[1] // uly
    kv_cols = keys.shape[1] // uly
    kv = jnp.concatenate(
        [keys.reshape(tokens, uly, kv_cols), values.reshape(tokens, uly, kv_cols)], axis=2
    )
    kv = lax.all_to_all(mirrored(kv, flip, cores), "uly", split_axis=1, concat_axis=0, tiled=True)
    rows = kv.shape[0]
    kv = kv.reshape(rows, 2 * kv_cols)
    window = [kv]
    for step in range(1, REACH + 1):
        source = window[1] if step == 2 else kv
        window.append(from_behind(source, 1 if step == 2 else step, flips, cores))
    packed = jnp.concatenate(
        [queries.reshape(tokens, uly, q_cols), output_gradient.reshape(tokens, uly, q_cols)],
        axis=2,
    )
    packed = mirrored(packed, flip, cores)
    packed = lax.all_to_all(packed, "uly", split_axis=1, concat_axis=0, tiled=True)
    packed = packed.reshape(rows, 2 * q_cols)
    queries = packed[:, :q_cols]
    gradient = packed[:, q_cols:]
    groups = q_cols // HEAD_SIZE
    softmax_scale = 1.0 / math.sqrt(HEAD_SIZE)

    window = jnp.concatenate(window[::-1], axis=0)
    key_window = window[:, :HEAD_SIZE]
    value_window = window[:, HEAD_SIZE:]

    q_base = ctx_index * rows
    k_base = (ctx_index - REACH) * rows
    q_pos = q_base + jnp.arange(rows, dtype=jnp.int32)
    ends = jnp.cumsum(doc_lengths)
    q_start = jnp.sum(
        jnp.where(ends[None, :] <= q_pos[:, None], doc_lengths[None, :], 0), axis=1
    ).astype(jnp.int32)
    first_rows = jnp.arange(0, rows, Q_BLOCK, dtype=jnp.int32)
    lo = jnp.maximum((q_start[first_rows] - k_base) // K_BLOCK, 0)
    hi = (q_base + first_rows + Q_BLOCK - 1 - k_base) // K_BLOCK + 1
    meta = jnp.concatenate(
        [jnp.stack([q_base, k_base]).astype(jnp.int32), jnp.stack([lo, hi], axis=1).reshape(-1)]
    ).astype(jnp.int32)

    dq, dk_window, dv_window = attend(
        meta, queries, gradient, key_window, value_window, q_start[:, None], groups, softmax_scale
    )
    partials = jnp.concatenate([dk_window, dv_window], axis=1)
    returned = [
        from_behind(
            partials[(REACH - step) * rows : (REACH - step + 1) * rows].astype(jnp.bfloat16),
            -step,
            flips,
            cores,
        )
        for step in range(1, REACH + 1)
    ]
    out_q = lax.all_to_all(dq, "uly", split_axis=0, concat_axis=1, tiled=True)
    out_q, returned = lax.optimization_barrier((out_q, returned))
    out_q = mirrored(out_q.reshape(out_q.shape[0], uly, q_cols), flip, cores)
    total = partials[REACH * rows :]
    for piece in returned:
        total = total + piece.astype(jnp.float32)
    out_k = (softmax_scale * total[:, :HEAD_SIZE]).astype(jnp.bfloat16)
    out_v = total[:, HEAD_SIZE:].astype(jnp.bfloat16)
    out_kv = lax.all_to_all(
        jnp.concatenate([out_k, out_v], axis=1), "uly", split_axis=0, concat_axis=1, tiled=True
    )
    out_kv = mirrored(out_kv.reshape(out_kv.shape[0], uly, 2 * kv_cols), flip, cores)
    return (
        out_q.reshape(out_q.shape[0], uly * q_cols),
        out_kv[:, :, :kv_cols].reshape(out_kv.shape[0], uly * kv_cols),
        out_kv[:, :, kv_cols:].reshape(out_kv.shape[0], uly * kv_cols),
    )


def layout_of(mesh):
    devices = mesh.devices
    cores = len({getattr(d, "core_on_chip", 0) for d in devices.flat})
    run = devices.shape[1] // cores
    coords = [getattr(devices[c, 0], "coords", None) for c in range(devices.shape[0])]
    if any(xyz is None for xyz in coords):
        return (False,) * devices.shape[0], cores
    return tuple(bool((xyz[2] // run) % 2) for xyz in coords), cores


def solution(mesh):
    flips, cores = layout_of(mesh)
    return jax.shard_map(
        functools.partial(on_device, flips=flips, cores=cores),
        mesh=mesh,
        in_specs=(
            P(("ctx", "uly"), None),
            P(("ctx", "uly"), None),
            P(("ctx", "uly"), None),
            P(("ctx", "uly"), None),
            P(),
        ),
        out_specs=(P(("ctx", "uly"), None), P(("ctx", "uly"), None), P(("ctx", "uly"), None)),
        check_vma=False,
    )
```

```python
import functools
import math

import jax
import jax.numpy as jnp
from jax import lax
from jax.experimental import pallas as pl
from jax.experimental.pallas import tpu as pltpu
from jax.sharding import PartitionSpec as P

HEAD_SIZE = 128
REACH = 3
Q_BLOCK = 512
K_BLOCK = 512

NEG = -1e30


def mirror_of(uly, cores):
    run = uly // cores
    return [(run - 1 - u // cores) * cores + u % cores for u in range(uly)]


def from_behind(shard, by, flips, cores):
    ctx = lax.axis_size("ctx")
    uly = lax.axis_size("uly")
    mirror = mirror_of(uly, cores)
    pairs = []
    for c in range(ctx):
        d = c + by
        if not 0 <= d < ctx:
            continue
        for u in range(uly):
            group = mirror[u] if flips[c] else u
            pairs.append((c * uly + u, d * uly + (mirror[group] if flips[d] else group)))
    return lax.ppermute(shard, ("ctx", "uly"), pairs)


def mirrored(x, flip, cores):
    rows, uly = x.shape[0], x.shape[1]
    split = x.reshape(rows, uly // cores, cores, x.shape[2])
    return jnp.where(flip, split[:, ::-1], split).reshape(x.shape)


def attention_kernel(
    meta_ref, q_ref, do_ref, k_ref, v_ref, qs_ref, qsr_ref,
    dq_ref, dk_ref, dv_ref,
    m_s, l_s, acc_s, lse_s, delta_s, dq_s,
    *, groups, q_blocks, scale,
):
    T, TK, D = Q_BLOCK, K_BLOCK, HEAD_SIZE
    nt = (((1,), (1,)), ((), ()))
    dk_ref[...] = jnp.zeros_like(dk_ref)
    dv_ref[...] = jnp.zeros_like(dv_ref)
    q_base = meta_ref[0]
    k_base = meta_ref[1]

    def q_block(qb, carry):
        q0 = pl.multiple_of(qb * T, T)
        lo = meta_ref[2 + 2 * qb]
        hi = meta_ref[3 + 2 * qb]
        m_s[...] = jnp.full_like(m_s, NEG)
        l_s[...] = jnp.zeros_like(l_s)
        acc_s[...] = jnp.zeros_like(acc_s)

        def fwd(kb, c):
            k0 = pl.multiple_of(kb * TK, TK)
            k = k_ref[pl.ds(k0, TK), :]
            v_t = v_ref[pl.ds(k0, TK), :].astype(jnp.float32).T.astype(jnp.bfloat16)
            k_pos = k_base + k0 + lax.broadcasted_iota(jnp.int32, (TK, T), 0)
            q_pos = q_base + q0 + lax.broadcasted_iota(jnp.int32, (TK, T), 1)
            start = qsr_ref[:, pl.ds(q0, T)]
            mask = (k_pos <= q_pos) & (k_pos >= start)
            for h in range(groups):
                qh = q_ref[pl.ds(q0, T), pl.ds(h * D, D)]
                raw = lax.dot_general(k, qh, nt, preferred_element_type=jnp.float32) * scale
                s = jnp.where(mask, raw, NEG)
                old_high = m_s[h]
                new_high = jnp.maximum(old_high, jnp.max(s, axis=0, keepdims=True))
                factor = jnp.exp(old_high - new_high)
                terms = jnp.exp(s - new_high)
                l_s[h] = l_s[h] * factor + jnp.sum(terms, axis=0, keepdims=True)
                acc_s[h] = acc_s[h] * factor + jnp.dot(
                    v_t, terms.astype(jnp.bfloat16), preferred_element_type=jnp.float32
                )
                m_s[h] = new_high
            return c

        lax.fori_loop(lo, hi, fwd, 0)
        for h in range(groups):
            total = l_s[h]
            lse_s[h] = m_s[h] + jnp.log(total)
            out = (acc_s[h] / total).astype(jnp.bfloat16).astype(jnp.float32)
            g = do_ref[pl.ds(q0, T), pl.ds(h * D, D)].astype(jnp.float32).T
            delta_s[h] = jnp.sum(g * out, axis=0, keepdims=True)
        dq_s[...] = jnp.zeros_like(dq_s)

        def bwd(kb, c):
            k0 = pl.multiple_of(kb * TK, TK)
            k = k_ref[pl.ds(k0, TK), :]
            v = v_ref[pl.ds(k0, TK), :]
            k_t = k.astype(jnp.float32).T.astype(jnp.bfloat16)
            k_pos = k_base + k0 + lax.broadcasted_iota(jnp.int32, (TK, T), 0)
            q_pos = q_base + q0 + lax.broadcasted_iota(jnp.int32, (TK, T), 1)
            start = qsr_ref[:, pl.ds(q0, T)]
            mask = (k_pos <= q_pos) & (k_pos >= start)
            add_k = jnp.zeros((TK, D), jnp.float32)
            add_v = jnp.zeros((TK, D), jnp.float32)
            for h in range(groups):
                qh = q_ref[pl.ds(q0, T), pl.ds(h * D, D)]
                gh = do_ref[pl.ds(q0, T), pl.ds(h * D, D)]
                raw = lax.dot_general(k, qh, nt, preferred_element_type=jnp.float32) * scale
                probs = jnp.where(mask, jnp.exp(raw - lse_s[h]), 0.0)
                dprobs = lax.dot_general(v, gh, nt, preferred_element_type=jnp.float32)
                dscores = (probs * (dprobs - delta_s[h])).astype(jnp.bfloat16)
                add_v = add_v + jnp.dot(
                    probs.astype(jnp.bfloat16), gh, preferred_element_type=jnp.float32
                )
                add_k = add_k + jnp.dot(dscores, qh, preferred_element_type=jnp.float32)
                dq_s[h] = dq_s[h] + jnp.dot(k_t, dscores, preferred_element_type=jnp.float32)
            dk_ref[pl.ds(k0, TK), :] = dk_ref[pl.ds(k0, TK), :] + add_k
            dv_ref[pl.ds(k0, TK), :] = dv_ref[pl.ds(k0, TK), :] + add_v
            return c

        lax.fori_loop(lo, hi, bwd, 0)
        for h in range(groups):
            dq_ref[pl.ds(q0, T), pl.ds(h * D, D)] = (scale * dq_s[h].T).astype(dq_ref.dtype)
        return carry

    lax.fori_loop(0, q_blocks, q_block, 0)


def attend(meta, queries, gradient, key_window, value_window, q_start, groups, scale):
    rows = queries.shape[0]
    width = key_window.shape[0]
    q_blocks = rows // Q_BLOCK
    vmem = pltpu.MemorySpace.VMEM
    kernel = functools.partial(
        attention_kernel, groups=groups, q_blocks=q_blocks, scale=scale
    )
    return pl.pallas_call(
        kernel,
        out_shape=(
            jax.ShapeDtypeStruct(queries.shape, jnp.bfloat16),
            jax.ShapeDtypeStruct((width, HEAD_SIZE), jnp.float32),
            jax.ShapeDtypeStruct((width, HEAD_SIZE), jnp.float32),
        ),
        in_specs=[pl.BlockSpec(memory_space=pltpu.MemorySpace.SMEM)]
        + [pl.BlockSpec(memory_space=vmem)] * 6,
        out_specs=[pl.BlockSpec(memory_space=vmem)] * 3,
        scratch_shapes=[
            pltpu.VMEM((groups, 1, Q_BLOCK), jnp.float32),
            pltpu.VMEM((groups, 1, Q_BLOCK), jnp.float32),
            pltpu.VMEM((groups, HEAD_SIZE, Q_BLOCK), jnp.float32),
            pltpu.VMEM((groups, 1, Q_BLOCK), jnp.float32),
            pltpu.VMEM((groups, 1, Q_BLOCK), jnp.float32),
            pltpu.VMEM((groups, HEAD_SIZE, Q_BLOCK), jnp.float32),
        ],
        compiler_params=pltpu.CompilerParams(vmem_limit_bytes=48 * 1024 * 1024),
    )(meta, queries, gradient, key_window, value_window, q_start, q_start.reshape(1, rows))


def on_device(queries, keys, values, output_gradient, doc_lengths, flips, cores):
    uly = lax.axis_size("uly")
    ctx_index = lax.axis_index("ctx")
    flip = jnp.asarray(flips)[ctx_index]
    tokens = queries.shape[0]
    q_cols = queries.shape[1] // uly
    kv_cols = keys.shape[1] // uly
    kv = jnp.concatenate(
        [keys.reshape(tokens, uly, kv_cols), values.reshape(tokens, uly, kv_cols)], axis=2
    )
    kv = lax.all_to_all(mirrored(kv, flip, cores), "uly", split_axis=1, concat_axis=0, tiled=True)
    rows = kv.shape[0]
    kv = kv.reshape(rows, 2 * kv_cols)
    window = [kv]
    for step in range(1, REACH + 1):
        source = window[1] if step == 2 else kv
        window.append(from_behind(source, 1 if step == 2 else step, flips, cores))
    packed = jnp.concatenate(
        [queries.reshape(tokens, uly, q_cols), output_gradient.reshape(tokens, uly, q_cols)],
        axis=2,
    )
    packed = mirrored(packed, flip, cores)
    packed = lax.all_to_all(packed, "uly", split_axis=1, concat_axis=0, tiled=True)
    packed = packed.reshape(rows, 2 * q_cols)
    queries = packed[:, :q_cols]
    gradient = packed[:, q_cols:]
    groups = q_cols // HEAD_SIZE
    softmax_scale = 1.0 / math.sqrt(HEAD_SIZE)

    window = jnp.concatenate(window[::-1], axis=0)
    key_window = window[:, :HEAD_SIZE]
    value_window = window[:, HEAD_SIZE:]

    q_base = ctx_index * rows
    k_base = (ctx_index - REACH) * rows
    q_pos = q_base + jnp.arange(rows, dtype=jnp.int32)
    ends = jnp.cumsum(doc_lengths)
    q_start = jnp.sum(
        jnp.where(ends[None, :] <= q_pos[:, None], doc_lengths[None, :], 0), axis=1
    ).astype(jnp.int32)
    first_rows = jnp.arange(0, rows, Q_BLOCK, dtype=jnp.int32)
    lo = jnp.maximum((q_start[first_rows] - k_base) // K_BLOCK, 0)
    hi = (q_base + first_rows + Q_BLOCK - 1 - k_base) // K_BLOCK + 1
    meta = jnp.concatenate(
        [jnp.stack([q_base, k_base]).astype(jnp.int32), jnp.stack([lo, hi], axis=1).reshape(-1)]
    ).astype(jnp.int32)

    dq, dk_window, dv_window = attend(
        meta, queries, gradient, key_window, value_window, q_start[:, None], groups, softmax_scale
    )
    partials = jnp.concatenate([dk_window, dv_window], axis=1)
    returned = []
    for step in range(1, REACH + 1):
        piece = partials[(REACH - step) * rows : (REACH - step + 1) * rows].astype(jnp.bfloat16)
        if step == 2:
            piece = from_behind(piece, -1, flips, cores)
        returned.append(from_behind(piece, -1 if step == 2 else -step, flips, cores))
    out_q = lax.all_to_all(dq, "uly", split_axis=0, concat_axis=1, tiled=True)
    out_q, returned = lax.optimization_barrier((out_q, returned))
    out_q = mirrored(out_q.reshape(out_q.shape[0], uly, q_cols), flip, cores)
    total = partials[REACH * rows :]
    for piece in returned:
        total = total + piece.astype(jnp.float32)
    out_k = (softmax_scale * total[:, :HEAD_SIZE]).astype(jnp.bfloat16)
    out_v = total[:, HEAD_SIZE:].astype(jnp.bfloat16)
    out_kv = lax.all_to_all(
        jnp.concatenate([out_k, out_v], axis=1), "uly", split_axis=0, concat_axis=1, tiled=True
    )
    out_kv = mirrored(out_kv.reshape(out_kv.shape[0], uly, 2 * kv_cols), flip, cores)
    return (
        out_q.reshape(out_q.shape[0], uly * q_cols),
        out_kv[:, :, :kv_cols].reshape(out_kv.shape[0], uly * kv_cols),
        out_kv[:, :, kv_cols:].reshape(out_kv.shape[0], uly * kv_cols),
    )


def layout_of(mesh):
    devices = mesh.devices
    cores = len({getattr(d, "core_on_chip", 0) for d in devices.flat})
    run = devices.shape[1] // cores
    coords = [getattr(devices[c, 0], "coords", None) for c in range(devices.shape[0])]
    if any(xyz is None for xyz in coords):
        return (False,) * devices.shape[0], cores
    return tuple(bool((xyz[2] // run) % 2) for xyz in coords), cores


def solution(mesh):
    flips, cores = layout_of(mesh)
    return jax.shard_map(
        functools.partial(on_device, flips=flips, cores=cores),
        mesh=mesh,
        in_specs=(
            P(("ctx", "uly"), None),
            P(("ctx", "uly"), None),
            P(("ctx", "uly"), None),
            P(("ctx", "uly"), None),
            P(),
        ),
        out_specs=(P(("ctx", "uly"), None), P(("ctx", "uly"), None), P(("ctx", "uly"), None)),
        check_vma=False,
    )
```

```python
import functools
import math

import jax
import jax.numpy as jnp
from jax import lax
from jax.experimental import pallas as pl
from jax.experimental.pallas import tpu as pltpu
from jax.sharding import PartitionSpec as P

HEAD_SIZE = 128
REACH = 3
Q_BLOCK = 512
K_BLOCK = 512

NEG = -1e30


def mirror_of(uly, cores):
    run = uly // cores
    return [(run - 1 - u // cores) * cores + u % cores for u in range(uly)]


def from_behind(shard, by, flips, cores):
    ctx = lax.axis_size("ctx")
    uly = lax.axis_size("uly")
    mirror = mirror_of(uly, cores)
    pairs = []
    for c in range(ctx):
        d = c + by
        if not 0 <= d < ctx:
            continue
        for u in range(uly):
            group = mirror[u] if flips[c] else u
            pairs.append((c * uly + u, d * uly + (mirror[group] if flips[d] else group)))
    return lax.ppermute(shard, ("ctx", "uly"), pairs)


def mirrored(x, flip, cores):
    rows, uly = x.shape[0], x.shape[1]
    split = x.reshape(rows, uly // cores, cores, x.shape[2])
    return jnp.where(flip, split[:, ::-1], split).reshape(x.shape)


def attention_kernel(
    meta_ref, q_ref, do_ref, k_ref, v_ref, qs_ref, qsr_ref,
    dq_ref, dkv_ref,
    m_s, l_s, acc_s, lse_s, delta_s, dq_s,
    *, groups, q_blocks, scale,
):
    T, TK, D = Q_BLOCK, K_BLOCK, HEAD_SIZE
    nt = (((1,), (1,)), ((), ()))
    dkv_ref[...] = jnp.zeros_like(dkv_ref)
    q_base = meta_ref[0]
    k_base = meta_ref[1]

    def q_block(qb, carry):
        q0 = pl.multiple_of(qb * T, T)
        lo = meta_ref[2 + 3 * qb]
        hi = meta_ref[3 + 3 * qb]
        last_start = meta_ref[4 + 3 * qb]
        m_s[...] = jnp.full_like(m_s, NEG)
        l_s[...] = jnp.zeros_like(l_s)
        acc_s[...] = jnp.zeros_like(acc_s)

        def tile_mask(k0):
            k_pos = k_base + k0 + lax.broadcasted_iota(jnp.int32, (TK, T), 0)
            q_pos = q_base + q0 + lax.broadcasted_iota(jnp.int32, (TK, T), 1)
            start = qsr_ref[:, pl.ds(q0, T)]
            return (k_pos <= q_pos) & (k_pos >= start)

        def is_full(k0):
            return (k_base + k0 + TK - 1 <= q_base + q0) & (k_base + k0 >= last_start)

        def fwd_tile(k0, masked):
            k = k_ref[pl.ds(k0, TK), :]
            v_t = v_ref[pl.ds(k0, TK), :].astype(jnp.float32).T.astype(jnp.bfloat16)
            mask = tile_mask(k0) if masked else None
            for h in range(groups):
                qh = q_ref[pl.ds(q0, T), pl.ds(h * D, D)]
                raw = lax.dot_general(k, qh, nt, preferred_element_type=jnp.float32) * scale
                s = jnp.where(mask, raw, NEG) if masked else raw
                old_high = m_s[h]
                new_high = jnp.maximum(old_high, jnp.max(s, axis=0, keepdims=True))
                factor = jnp.exp(old_high - new_high)
                terms = jnp.exp(s - new_high)
                l_s[h] = l_s[h] * factor + jnp.sum(terms, axis=0, keepdims=True)
                acc_s[h] = acc_s[h] * factor + jnp.dot(
                    v_t, terms.astype(jnp.bfloat16), preferred_element_type=jnp.float32
                )
                m_s[h] = new_high

        def fwd(kb, c):
            k0 = pl.multiple_of(kb * TK, TK)
            full = is_full(k0)
            pl.when(full)(lambda: fwd_tile(k0, False))
            pl.when(jnp.logical_not(full))(lambda: fwd_tile(k0, True))
            return c

        lax.fori_loop(lo, hi, fwd, 0)
        for h in range(groups):
            total = l_s[h]
            lse_s[h] = m_s[h] + jnp.log(total)
            out = (acc_s[h] / total).astype(jnp.bfloat16).astype(jnp.float32)
            g = do_ref[pl.ds(q0, T), pl.ds(h * D, D)].astype(jnp.float32).T
            delta_s[h] = jnp.sum(g * out, axis=0, keepdims=True)
        dq_s[...] = jnp.zeros_like(dq_s)

        def bwd_tile(k0, masked):
            k = k_ref[pl.ds(k0, TK), :]
            v = v_ref[pl.ds(k0, TK), :]
            k_t = k.astype(jnp.float32).T.astype(jnp.bfloat16)
            mask = tile_mask(k0) if masked else None
            add_k = jnp.zeros((TK, D), jnp.float32)
            add_v = jnp.zeros((TK, D), jnp.float32)
            for h in range(groups):
                qh = q_ref[pl.ds(q0, T), pl.ds(h * D, D)]
                gh = do_ref[pl.ds(q0, T), pl.ds(h * D, D)]
                raw = lax.dot_general(k, qh, nt, preferred_element_type=jnp.float32) * scale
                probs = jnp.exp(raw - lse_s[h])
                if masked:
                    probs = jnp.where(mask, probs, 0.0)
                dprobs = lax.dot_general(v, gh, nt, preferred_element_type=jnp.float32)
                dscores = (probs * (dprobs - delta_s[h])).astype(jnp.bfloat16)
                add_v = add_v + jnp.dot(
                    probs.astype(jnp.bfloat16), gh, preferred_element_type=jnp.float32
                )
                add_k = add_k + jnp.dot(dscores, qh, preferred_element_type=jnp.float32)
                dq_s[h] = dq_s[h] + jnp.dot(k_t, dscores, preferred_element_type=jnp.float32)
            dkv_ref[pl.ds(k0, TK), pl.ds(0, D)] = dkv_ref[pl.ds(k0, TK), pl.ds(0, D)] + add_k
            dkv_ref[pl.ds(k0, TK), pl.ds(D, D)] = dkv_ref[pl.ds(k0, TK), pl.ds(D, D)] + add_v

        def bwd(kb, c):
            k0 = pl.multiple_of(kb * TK, TK)
            full = is_full(k0)
            pl.when(full)(lambda: bwd_tile(k0, False))
            pl.when(jnp.logical_not(full))(lambda: bwd_tile(k0, True))
            return c

        lax.fori_loop(lo, hi, bwd, 0)
        for h in range(groups):
            dq_ref[pl.ds(q0, T), pl.ds(h * D, D)] = (scale * dq_s[h].T).astype(dq_ref.dtype)
        return carry

    lax.fori_loop(0, q_blocks, q_block, 0)


def attend(meta, queries, gradient, key_window, value_window, q_start, groups, scale):
    rows = queries.shape[0]
    width = key_window.shape[0]
    q_blocks = rows // Q_BLOCK
    vmem = pltpu.MemorySpace.VMEM
    kernel = functools.partial(
        attention_kernel, groups=groups, q_blocks=q_blocks, scale=scale
    )
    return pl.pallas_call(
        kernel,
        out_shape=(
            jax.ShapeDtypeStruct(queries.shape, jnp.bfloat16),
            jax.ShapeDtypeStruct((width, 2 * HEAD_SIZE), jnp.float32),
        ),
        in_specs=[pl.BlockSpec(memory_space=pltpu.MemorySpace.SMEM)]
        + [pl.BlockSpec(memory_space=vmem)] * 6,
        out_specs=[pl.BlockSpec(memory_space=vmem)] * 2,
        scratch_shapes=[
            pltpu.VMEM((groups, 1, Q_BLOCK), jnp.float32),
            pltpu.VMEM((groups, 1, Q_BLOCK), jnp.float32),
            pltpu.VMEM((groups, HEAD_SIZE, Q_BLOCK), jnp.float32),
            pltpu.VMEM((groups, 1, Q_BLOCK), jnp.float32),
            pltpu.VMEM((groups, 1, Q_BLOCK), jnp.float32),
            pltpu.VMEM((groups, HEAD_SIZE, Q_BLOCK), jnp.float32),
        ],
        compiler_params=pltpu.CompilerParams(vmem_limit_bytes=48 * 1024 * 1024),
    )(meta, queries, gradient, key_window, value_window, q_start, q_start.reshape(1, rows))


def on_device(queries, keys, values, output_gradient, doc_lengths, flips, cores):
    uly = lax.axis_size("uly")
    ctx_index = lax.axis_index("ctx")
    flip = jnp.asarray(flips)[ctx_index]
    tokens = queries.shape[0]
    q_cols = queries.shape[1] // uly
    kv_cols = keys.shape[1] // uly
    kv = jnp.concatenate(
        [keys.reshape(tokens, uly, kv_cols), values.reshape(tokens, uly, kv_cols)], axis=2
    )
    kv = lax.all_to_all(mirrored(kv, flip, cores), "uly", split_axis=1, concat_axis=0, tiled=True)
    rows = kv.shape[0]
    kv = kv.reshape(rows, 2 * kv_cols)
    window = [kv]
    for step in range(1, REACH + 1):
        source = window[1] if step == 2 else kv
        window.append(from_behind(source, 1 if step == 2 else step, flips, cores))
    packed = jnp.concatenate(
        [queries.reshape(tokens, uly, q_cols), output_gradient.reshape(tokens, uly, q_cols)],
        axis=2,
    )
    packed = mirrored(packed, flip, cores)
    packed = lax.all_to_all(packed, "uly", split_axis=1, concat_axis=0, tiled=True)
    packed = packed.reshape(rows, 2 * q_cols)
    queries = packed[:, :q_cols]
    gradient = packed[:, q_cols:]
    groups = q_cols // HEAD_SIZE
    softmax_scale = 1.0 / math.sqrt(HEAD_SIZE)

    window = jnp.concatenate(window[::-1], axis=0)
    key_window = window[:, :HEAD_SIZE]
    value_window = window[:, HEAD_SIZE:]

    q_base = ctx_index * rows
    k_base = (ctx_index - REACH) * rows
    q_pos = q_base + jnp.arange(rows, dtype=jnp.int32)
    ends = jnp.cumsum(doc_lengths)
    q_start = jnp.sum(
        jnp.where(ends[None, :] <= q_pos[:, None], doc_lengths[None, :], 0), axis=1
    ).astype(jnp.int32)
    first_rows = jnp.arange(0, rows, Q_BLOCK, dtype=jnp.int32)
    lo = jnp.maximum((q_start[first_rows] - k_base) // K_BLOCK, 0)
    hi = (q_base + first_rows + Q_BLOCK - 1 - k_base) // K_BLOCK + 1
    meta = jnp.concatenate(
        [jnp.stack([q_base, k_base]).astype(jnp.int32), jnp.stack([lo, hi, q_start[first_rows + Q_BLOCK - 1]], axis=1).reshape(-1)]
    ).astype(jnp.int32)

    dq, partials = attend(
        meta, queries, gradient, key_window, value_window, q_start[:, None], groups, softmax_scale
    )
    returned = [
        from_behind(
            partials[(REACH - step) * rows : (REACH - step + 1) * rows].astype(jnp.bfloat16),
            -step,
            flips,
            cores,
        )
        for step in range(1, REACH + 1)
    ]
    out_q = lax.all_to_all(dq, "uly", split_axis=0, concat_axis=1, tiled=True)
    out_q, returned = lax.optimization_barrier((out_q, returned))
    out_q = mirrored(out_q.reshape(out_q.shape[0], uly, q_cols), flip, cores)
    total = partials[REACH * rows :]
    for piece in returned:
        total = total + piece.astype(jnp.float32)
    out_k = (softmax_scale * total[:, :HEAD_SIZE]).astype(jnp.bfloat16)
    out_v = total[:, HEAD_SIZE:].astype(jnp.bfloat16)
    out_kv = lax.all_to_all(
        jnp.concatenate([out_k, out_v], axis=1), "uly", split_axis=0, concat_axis=1, tiled=True
    )
    out_kv = mirrored(out_kv.reshape(out_kv.shape[0], uly, 2 * kv_cols), flip, cores)
    return (
        out_q.reshape(out_q.shape[0], uly * q_cols),
        out_kv[:, :, :kv_cols].reshape(out_kv.shape[0], uly * kv_cols),
        out_kv[:, :, kv_cols:].reshape(out_kv.shape[0], uly * kv_cols),
    )


def layout_of(mesh):
    devices = mesh.devices
    cores = len({getattr(d, "core_on_chip", 0) for d in devices.flat})
    run = devices.shape[1] // cores
    coords = [getattr(devices[c, 0], "coords", None) for c in range(devices.shape[0])]
    if any(xyz is None for xyz in coords):
        return (False,) * devices.shape[0], cores
    return tuple(bool((xyz[2] // run) % 2) for xyz in coords), cores


def solution(mesh):
    flips, cores = layout_of(mesh)
    return jax.shard_map(
        functools.partial(on_device, flips=flips, cores=cores),
        mesh=mesh,
        in_specs=(
            P(("ctx", "uly"), None),
            P(("ctx", "uly"), None),
            P(("ctx", "uly"), None),
            P(("ctx", "uly"), None),
            P(),
        ),
        out_specs=(P(("ctx", "uly"), None), P(("ctx", "uly"), None), P(("ctx", "uly"), None)),
        check_vma=False,
    )
```
